128 devices in a mesh: ctx: 32 (over y, z, core), head: 4 (over x).
Axes of the slice: x: 4, y: 4, z: 4, core: 2. Of those that a mesh axis runs over, the one named last changes fastest.
Arguments:
- mixer_input: bfloat16 [2, 8192, 8192], P(None, 'ctx', 'head'), may hold values from -6 to 6
- gate_input: bfloat16 [2, 8192, 8192], P(None, 'ctx', 'head'), may hold values from -6 to 6
- state_in: bfloat16 [2, 8192, 1024], P(None, 'ctx', 'head'), may hold values from -0.875 to 0.875
- state_out: bfloat16 [2, 8192, 1024], P(None, 'ctx', 'head'), may hold values from -0.875 to 0.875
- step_sizes: float32 [2, 8192, 128], P(None, 'ctx', 'head'), may hold values from 0.5 to 2
- decay_rates: float32 [128], P('head'), may hold values from 3.0517578e-05 to 0.05
- skip_gain: float32 [128], P('head'), may hold values from 0.5 to 2
- norm_gain: float32 [8192], P('head'), may hold values from 0.5 to 1.5
- out_weight: bfloat16 [8192, 4096], P('head', 'ctx'), may hold values from -0.0625 to 0.0625
- queries: bfloat16 [2, 8192, 4096], P(None, 'ctx', 'head'), may hold values from -4.375 to 4.375
- keys: bfloat16 [2, 8192, 1024], P(None, 'ctx', 'head'), may hold values from -4.375 to 4.375
- values: bfloat16 [2, 8192, 1024], P(None, 'ctx', 'head'), may hold values from -6 to 6
- doc_ids: int32 [2, 8192], P(None, 'ctx'), may hold values from 0 to 15, never falling along the last dimension, each value on 1 to 1024 neighbouring positions
Outputs:
- mixer_out: bfloat16 [2, 8192, 4096], P(None, 'ctx', 'head')
- attn_out: bfloat16 [2, 8192, 4096], P(None, 'ctx', 'head')
The draws below stay inside these ranges and needn't reach their ends.
Inputs may be any that keep to these rules, and one draw needn't show every extreme that they name: `doc_ids`: along each sequence the ids never fall and every id occurs; each document has 1 to 1024 positions, and one document of each sequence has exactly 1024.
All inputs are finite; a program needn't handle non-finite values.
Results may differ from the reference program's by a relative error of at most 0.014.
Values may be sent and summed in bfloat16 or wider, within the bound.
No kernel may reach another device: no remote copies, remote signals or barrier semaphores. Data moves between devices by JAX's collectives and lax.ppermute only.
A program may use at most 256 MiB of HBM per device.

```python
import math
import jax
import jax.numpy as jnp
import numpy as np
from jax import lax

D = 4096
H = 128
P_SIZE = 64
N = 128
G = 8
QH = 32
KH = 8
HD = 128
SPAN = 128
DOCS = 16
BATCH = 2
SEQ_DEV = 256
SEQ = 8192
INNER = 8192
HEAD_DEV = 32
REACH = 4


def draw_queries(key, part):
    drawn = jax.random.normal(jax.random.fold_in(key, 1), (BATCH, SEQ, QH, HD), jnp.float32)
    drawn = jnp.clip(drawn, -4.375, 4.375)
    return drawn.reshape(BATCH, SEQ, QH * HD).astype(jnp.bfloat16)


def draw_keys(key, part):
    drawn = jax.random.normal(jax.random.fold_in(key, 2), (BATCH, SEQ, KH, HD), jnp.float32)
    drawn = jnp.clip(drawn, -4.375, 4.375)
    return drawn.reshape(BATCH, SEQ, KH * HD).astype(jnp.bfloat16)


def shard_levels(own_key, shape, shards, least, high):
    factor_of, own = 1.0, jax.random.fold_in(own_key, 6)
    for position, blocks in shards:
        heights = jnp.exp(jax.random.uniform(jax.random.fold_in(own, position), (blocks,), jnp.float32, least / len(shards), high / len(shards)))
        factor_of = factor_of * jnp.repeat(heights, shape[position] // blocks).reshape([-1 if axis == position else 1 for axis in range(len(shape))])
    return factor_of


def split_up(count, total, limit, lean):
    portions = [(1 << 20) // math.isqrt(standing ** lean) + 1 for standing in range(2, count + 1)]
    rest, counts = total - limit - (count - 1), [1] * (count - 1)
    while rest > 0:
        free = [i for i in range(count - 1) if counts[i] < limit]
        whole, left = sum([portions[i] for i in free]), rest
        for i in free:
            extra = min(limit - counts[i], max(1, left * portions[i] // whole), rest)
            counts[i] = counts[i] + extra
            rest = rest - extra
    return np.array([limit] + counts)


def ragged(stream_key, number_of, total, most, lean):
    if number_of == 2:
        one = jax.random.randint(stream_key, (), max(1, total - most), min(most, total - 1) + 1)
        return jnp.stack([one, total - one])
    sizes = jnp.asarray(split_up(number_of, total, most, lean), jnp.int32)
    couples = (number_of - 1) // 2
    giver, receiver = sizes[1:1 + 2 * couples:2], sizes[2:2 + 2 * couples:2]
    room = jnp.minimum(giver - 1, most - receiver)
    moved = jax.random.randint(jax.random.fold_in(stream_key, 1), (couples,), 0, 1 << 20) % (room + 1)
    sizes = sizes.at[1:1 + 2 * couples:2].set(giver - moved).at[2:2 + 2 * couples:2].set(receiver + moved)
    return sizes[jax.random.permutation(jax.random.fold_in(stream_key, 2), number_of)]


def normal_values(key, extent, deviation, limit, shards=(), kind=jnp.bfloat16):
    values = jax.random.normal(key, extent, jnp.float32) * deviation
    if len(shards) > 0:
        values = shard_levels(key, extent, shards, -0.22, 0.18) * values
    return jnp.clip(values, min=-limit, max=limit).astype(kind)


def setup_inputs(seed: int = 0) -> dict:
    seeds = jax.random.split(jax.random.key(seed), 14)
    mixer_input = normal_values(seeds[0], (BATCH, SEQ, INNER), 1.0, 6.0, ((1, 32), (2, 4)))
    gate_input = normal_values(seeds[1], (BATCH, SEQ, INNER), 1.0, 6.0, ((1, 32), (2, 4)))
    state_in = normal_values(seeds[2], (BATCH, SEQ, G * N), 0.15, 0.875, ((1, 32), (2, 4)))
    state_out = normal_values(seeds[3], (BATCH, SEQ, G * N), 0.15, 0.875, ((1, 32), (2, 4)))
    step_sizes = jnp.clip(jnp.exp(math.log(2.0) - 1.3862944 * jax.random.uniform(seeds[4], (BATCH, SEQ, H), jnp.float32) ** shard_levels(seeds[4], (BATCH, SEQ, H), ((1, 32), (2, 4)), -0.2, 0.2)), 0.5, 2.0)
    decay_rates = jnp.clip(jnp.exp(math.log(0.05) - 7.4014754 * jax.random.uniform(seeds[5], (H,), jnp.float32) ** shard_levels(seeds[5], (H,), ((0, 4),), -0.2, 0.2)), 3.0517578125e-05, 0.05)
    skip_gain = jnp.clip(0.5 + 1.5 * jax.random.uniform(seeds[6], (H,), jnp.float32) ** shard_levels(seeds[6], (H,), ((0, 4),), -0.2, 0.2), 0.5, 2.0)
    norm_gain = jnp.clip(1.0 + 0.1 * jax.random.normal(seeds[7], (INNER,), jnp.float32), 0.5, 1.5)
    out_weight = normal_values(seeds[8], (INNER, D), INNER ** -0.5, 0.0625, ((0, 4), (1, 32)))
    queries = draw_queries(jax.random.fold_in(seeds[13], 71), 0)
    keys = draw_keys(jax.random.fold_in(seeds[13], 71), 0)
    values = normal_values(seeds[11], (BATCH, SEQ, KH * HD), 1.0, 6.0, ((1, 32), (2, 4)))
    doc_ids = jax.vmap(lambda own: jnp.searchsorted(jnp.cumsum(ragged(own, DOCS, SEQ, SEQ // 8, 2)), jnp.arange(SEQ), side="right"))(jax.random.split(seeds[12], BATCH)).reshape((BATCH, SEQ)).astype(jnp.int32)
    return dict(mixer_input=mixer_input, gate_input=gate_input, state_in=state_in, state_out=state_out, step_sizes=step_sizes, decay_rates=decay_rates, skip_gain=skip_gain, norm_gain=norm_gain, out_weight=out_weight, queries=queries, keys=keys, values=values, doc_ids=doc_ids)


epsilon = 1e-05
lowest = -1e+30

def span_scan(inputs, widths, rates, writers, readers, documents, block, initial, initial_doc):
    batches, length, heads, channels = inputs.shape
    groups = writers.shape[2]
    repeat = heads // groups
    count = length // block

    def split(array):
        shaped = array.reshape((batches, count, block) + array.shape[2:])
        return jnp.moveaxis(shaped, 1, 0)
    order = jnp.arange(block, dtype=jnp.int32)
    causal = order[:, None] >= order[None, :]

    def advance(carry, pieces):
        state, state_doc = carry
        input_now, width_now, writer_now, reader_now, doc_now = pieces
        cumulative = jnp.cumsum(width_now * rates, axis=1)
        allowed = ((doc_now[:, :, None] == doc_now[:, None, :]) & causal)[..., None]
        spread = cumulative[:, :, None, :] - cumulative[:, None, :, :]
        decays = jnp.where(allowed, jnp.exp(-jnp.where(allowed, spread, 0.0)), 0.0)
        intersection = jnp.einsum('btgn,bsgn->btsg', reader_now, writer_now, preferred_element_type=jnp.float32)
        intersection = jnp.repeat(intersection, repeat, axis=3)
        mixing = (decays * intersection * width_now[:, None, :, :]).astype(jnp.bfloat16)
        within = jnp.einsum('btsh,bshp->bthp', mixing, input_now, preferred_element_type=jnp.float32)
        read_heads = jnp.repeat(reader_now, repeat, axis=2)
        living = (doc_now == state_doc[:, None]).astype(jnp.float32)
        carried = jnp.einsum('bthn,bhpn->bthp', read_heads, state.astype(jnp.bfloat16), preferred_element_type=jnp.float32)
        carried = carried * (jnp.exp(-cumulative) * living[:, :, None])[..., None]
        last_doc = doc_now[:, -1]
        ending = cumulative[:, -1:, :] - cumulative
        tailing = jnp.where((doc_now == last_doc[:, None])[..., None], jnp.exp(-ending), 0.0) * width_now
        write_heads = jnp.repeat(writer_now, repeat, axis=2)
        keeping = jnp.exp(-cumulative[:, -1, :]) * (last_doc == state_doc).astype(jnp.float32)[:, None]
        scaled = (tailing[..., None] * input_now.astype(jnp.float32)).astype(jnp.bfloat16)
        written = jnp.einsum('bshp,bshn->bhpn', scaled, write_heads, preferred_element_type=jnp.float32)
        state = state * keeping[:, :, None, None] + written
        return ((state, last_doc), within + carried)
    pieces = (split(inputs), split(widths), split(writers), split(readers), split(documents))
    (state, last_doc), outputs = lax.scan(advance, (initial, initial_doc), pieces)
    outputs = jnp.moveaxis(outputs, 0, 1).reshape(batches, length, heads, channels)
    return (outputs, state)

def gate_norm(gated, gain, groups):
    shaped = gated.reshape(gated.shape[:-1] + (groups, gated.shape[-1] // groups))
    factor = lax.rsqrt(lax.optimization_barrier(jnp.mean(shaped * shaped, axis=-1, keepdims=True)) + epsilon)
    return ((shaped * factor).reshape(gated.shape) * gain).astype(jnp.bfloat16)

def attention(queries, keys, values, doc_ids):
    repeat = QH // KH
    query_heads = queries.reshape(BATCH, SEQ, KH, repeat, HD)
    key_heads = keys.reshape(BATCH, SEQ, KH, HD)
    value_heads = values.reshape(BATCH, SEQ, KH, HD)
    window = (REACH + 1) * SEQ_DEV
    scale = HD ** (-0.5)

    def one_block(index):
        query_start = (index * SEQ_DEV).astype(jnp.int32)
        key_start = jnp.maximum(query_start - REACH * SEQ_DEV, 0).astype(jnp.int32)
        query_block = lax.dynamic_slice_in_dim(query_heads, query_start, SEQ_DEV, 1)
        key_block = lax.dynamic_slice_in_dim(key_heads, key_start, window, 1)
        value_block = lax.dynamic_slice_in_dim(value_heads, key_start, window, 1)
        query_docs = lax.dynamic_slice_in_dim(doc_ids, query_start, SEQ_DEV, 1)
        key_docs = lax.dynamic_slice_in_dim(doc_ids, key_start, window, 1)
        query_pos = query_start + jnp.arange(SEQ_DEV, dtype=jnp.int32)
        key_pos = key_start + jnp.arange(window, dtype=jnp.int32)
        scores = jnp.einsum('bqgrd,bkgd->bgrqk', query_block.astype(jnp.float32), key_block.astype(jnp.float32), precision=lax.Precision.HIGHEST) * scale
        allowed = (key_pos[None, :] <= query_pos[:, None])[None] & (key_docs[:, None, :] == query_docs[:, :, None])
        allowed = allowed[:, None, None]
        top = lax.optimization_barrier(jnp.max(jnp.where(allowed, scores, lowest), axis=-1, keepdims=True))
        probs = jnp.where(allowed, jnp.exp(scores - top), 0.0)
        total = lax.optimization_barrier(jnp.sum(probs, axis=-1))
        weights = probs.astype(jnp.bfloat16)
        mixed = jnp.einsum('bgrqk,bkgd->bgrqd', weights.astype(jnp.float32), value_block.astype(jnp.float32), precision=lax.Precision.HIGHEST)
        result = mixed / total[..., None]
        return jnp.transpose(result, (0, 3, 1, 2, 4)).astype(jnp.bfloat16)
    blocks = lax.map(one_block, jnp.arange(SEQ // SEQ_DEV, dtype=jnp.int32))
    blocks = jnp.moveaxis(blocks, 0, 1)
    return blocks.reshape(BATCH, SEQ, QH * HD)

def reference(mixer_input, gate_input, state_in, state_out, step_sizes, decay_rates, skip_gain, norm_gain, out_weight, queries, keys, values, doc_ids):
    inputs = mixer_input.reshape(BATCH, SEQ, H, P_SIZE)
    writers = state_in.reshape(BATCH, SEQ, G, N)
    readers = state_out.reshape(BATCH, SEQ, G, N)
    initial = jnp.zeros((BATCH, H, P_SIZE, N), jnp.float32)
    initial_doc = jnp.full((BATCH,), -1, jnp.int32)
    scanned, _ = span_scan(inputs, step_sizes, decay_rates, writers, readers, doc_ids, SPAN, initial, initial_doc)
    mixed = scanned + skip_gain[:, None] * inputs.astype(jnp.float32)
    gated = mixed.reshape(BATCH, SEQ, H * P_SIZE) * jax.nn.silu(gate_input.astype(jnp.float32))
    normed = gate_norm(gated, norm_gain, G).reshape(BATCH * SEQ, H * P_SIZE)
    rows = HEAD_DEV * P_SIZE
    summed = jnp.zeros((BATCH * SEQ, D), jnp.float32)
    for index in range(H // HEAD_DEV):
        partial_value = jnp.dot(normed[:, index * rows:(index + 1) * rows], out_weight[index * rows:(index + 1) * rows], preferred_element_type=jnp.float32)
        summed = summed + lax.optimization_barrier(partial_value.astype(jnp.bfloat16)).astype(jnp.float32)
    mixer_out = summed.reshape(BATCH, SEQ, D).astype(jnp.bfloat16)
    attn_out = attention(queries, keys, values, doc_ids)
    return (mixer_out, attn_out)
```

```python
import jax
import jax.numpy as jnp
from jax import lax
from jax.sharding import PartitionSpec as P

P_SIZE = 64
N = 128
HD = 128
SPAN = 128


epsilon = 1e-05
lowest = -1e30


def shifted(value, axis, by):
    devices = lax.axis_size(axis)
    pairs = [(i, i + by) for i in range(devices) if 0 <= i + by < devices]
    return lax.ppermute(value, axis, pairs)


def link_states(earlier, later):
    decay_one, state_one, first_one, last_one = earlier
    decay_two, state_two, first_two, last_two = later
    passes = ((last_one == first_two) | (last_one < 0.0) | (first_two < 0.0)).astype(jnp.float32)
    through = passes[:, None] * decay_two
    decay = decay_one * through
    state = state_two + through[:, :, None, None] * state_one
    first = jnp.where(first_one < 0.0, first_two, first_one)
    last = jnp.where(last_two < 0.0, last_one, last_two)
    return (decay, state, first, last)


def shards(
    mixer_input,
    gate_input,
    state_in,
    state_out,
    step_sizes,
    decay_rates,
    skip_gain,
    norm_gain,
    out_weight,
    queries,
    keys,
    values,
    doc_ids,
):
    f32 = jnp.float32
    bf16 = jnp.bfloat16
    batches, length, channels = mixer_input.shape
    heads = step_sizes.shape[2]
    groups = state_in.shape[2] // N
    repeat = heads // groups
    count = length // SPAN
    reach = lax.axis_size("ctx") // 8
    position = lax.axis_index("ctx")

    doc_send = doc_ids.astype(bf16)
    arrivals = []
    for offset in range(reach, 0, -1):
        arrivals.append(shifted((keys, values, doc_send), "ctx", offset))

    x = mixer_input.reshape(batches, count, SPAN, heads, P_SIZE)
    dt = step_sizes.reshape(batches, count, SPAN, heads)
    docs = doc_ids.reshape(batches, count, SPAN)
    writers = state_in.reshape(batches, count, SPAN, groups, N)
    readers = state_out.reshape(batches, count, SPAN, groups, N)
    cum = jnp.cumsum(dt * decay_rates, axis=2)
    order = jnp.arange(SPAN, dtype=jnp.int32)
    causal = order[:, None] >= order[None, :]
    allowed = ((docs[:, :, :, None] == docs[:, :, None, :]) & causal)[:, :, None]
    cum_h = jnp.moveaxis(cum, 3, 2)
    spread = cum_h[..., :, None] - cum_h[..., None, :]
    decays = jnp.where(allowed, jnp.exp(-jnp.where(allowed, spread, 0.0)), 0.0)
    intersection = jnp.einsum(
        "bktgn,bksgn->bkgts", readers, writers, preferred_element_type=f32
    )
    intersection = jnp.repeat(intersection, repeat, axis=2)
    dt_h = jnp.moveaxis(dt, 3, 2)
    mixing = (decays * intersection * dt_h[:, :, :, None, :]).astype(bf16)
    within = jnp.einsum(
        "bkhts,bkshp->bkthp", mixing, x, preferred_element_type=f32
    )

    last_doc = docs[:, :, -1]
    ending = cum[:, :, -1:, :] - cum
    tailing = jnp.where((docs == last_doc[:, :, None])[..., None], jnp.exp(-ending), 0.0) * dt
    scaled = (tailing[..., None] * x.astype(f32)).astype(bf16)
    scaled = scaled.reshape(batches, count, SPAN, groups, repeat, P_SIZE)
    written = jnp.einsum(
        "bksgrp,bksgn->bkgrpn", scaled, writers, preferred_element_type=f32
    )
    totals = cum[:, :, -1, :]

    state = written[:, 0]
    block_outs = [within[:, 0]]
    for index in range(1, count):
        living = (docs[:, index] == last_doc[:, index - 1][:, None]).astype(f32)
        carried = jnp.einsum(
            "btgn,bgrpn->btgrp",
            readers[:, index],
            state.astype(bf16),
            preferred_element_type=f32,
        ).reshape(batches, SPAN, heads, P_SIZE)
        carried = carried * (jnp.exp(-cum[:, index]) * living[:, :, None])[..., None]
        block_outs.append(within[:, index] + carried)
        keeping = jnp.exp(-totals[:, index]) * (
            last_doc[:, index] == last_doc[:, index - 1]
        ).astype(f32)[:, None]
        state = state * keeping.reshape(batches, groups, repeat)[..., None, None] + written[:, index]
    local_out = jnp.stack(block_outs, axis=1).reshape(batches, length, heads, P_SIZE)

    cumulative = jnp.cumsum(step_sizes * decay_rates, axis=1)
    first_doc = doc_ids[:, 0]
    end_doc = doc_ids[:, -1]
    passing = jnp.exp(-cumulative[:, -1, :]) * (first_doc == end_doc).astype(f32)[:, None]
    own_state = state.reshape(batches, heads, P_SIZE, N)
    small = jnp.concatenate(
        [passing, first_doc.astype(f32)[:, None], end_doc.astype(f32)[:, None]], axis=1
    )
    received = []
    for offset in range(reach, 0, -1):
        got_small, got_state = shifted((small, own_state.astype(bf16)), "ctx", offset)
        received.append(
            (got_small[:, :heads], got_state.astype(f32), got_small[:, heads], got_small[:, heads + 1])
        )
    before = received[0]
    for item in received[1:]:
        before = link_states(before, item)

    living = (doc_ids.astype(f32) == before[3][:, None]).astype(f32)
    carried = jnp.einsum(
        "btgn,bgrpn->btgrp",
        state_out.reshape(batches, length, groups, N),
        before[1].astype(bf16).reshape(batches, groups, repeat, P_SIZE, N),
        preferred_element_type=f32,
    ).reshape(batches, length, heads, P_SIZE)
    carried = carried * (jnp.exp(-cumulative) * living[:, :, None])[..., None]
    inputs = mixer_input.reshape(batches, length, heads, P_SIZE)
    mixed = local_out + carried + skip_gain[:, None] * inputs.astype(f32)
    gated = mixed.reshape(batches, length, channels) * jax.nn.silu(gate_input.astype(f32))
    shaped = gated.reshape(batches, length, groups, channels // groups)
    factor = lax.rsqrt(jnp.mean(shaped * shaped, axis=-1, keepdims=True) + epsilon)
    normed = ((shaped * factor).reshape(batches, length, channels) * norm_gain).astype(bf16)
    projected = jnp.einsum(
        "btc,cd->btd",
        normed,
        lax.all_gather(out_weight, "ctx", axis=1, tiled=True),
        preferred_element_type=f32,
    )
    mixer_out = lax.psum_scatter(
        projected.astype(bf16), "head", scatter_dimension=2, tiled=True
    )

    kv_heads = keys.shape[2] // HD
    q_repeat = queries.shape[2] // HD // kv_heads
    query_heads = queries.reshape(batches, length, kv_heads, q_repeat, HD)
    window_keys = jnp.concatenate([a[0] for a in arrivals] + [keys], axis=1)
    window_values = jnp.concatenate([a[1] for a in arrivals] + [values], axis=1)
    key_docs = []
    for index, item in enumerate(arrivals):
        offset = reach - index
        key_docs.append(jnp.where(position >= offset, item[2].astype(jnp.int32), -1))
    key_docs = jnp.concatenate(key_docs + [doc_ids], axis=1)
    window = (reach + 1) * length
    query_pos = reach * length + jnp.arange(length, dtype=jnp.int32)
    key_pos = jnp.arange(window, dtype=jnp.int32)
    key_heads = window_keys.reshape(batches, window, kv_heads, HD)
    value_heads = window_values.reshape(batches, window, kv_heads, HD)
    scale = HD ** (-0.5)
    scores = (
        jnp.einsum("bqgrd,bkgd->bgrqk", query_heads, key_heads, preferred_element_type=f32)
        * scale
    )
    allowed = (key_pos[None, :] <= query_pos[:, None])[None] & (
        key_docs[:, None, :] == doc_ids[:, :, None]
    )
    allowed = allowed[:, None, None]
    top = jnp.max(jnp.where(allowed, scores, lowest), axis=-1, keepdims=True)
    probs = jnp.where(allowed, jnp.exp(scores - top), 0.0)
    total = jnp.sum(probs, axis=-1)
    mixed_values = jnp.einsum(
        "bgrqk,bkgd->bgrqd", probs.astype(bf16), value_heads, preferred_element_type=f32
    )
    result = mixed_values / total[..., None]
    attn_out = (
        jnp.transpose(result, (0, 3, 1, 2, 4))
        .reshape(batches, length, kv_heads * q_repeat * HD)
        .astype(bf16)
    )
    return (mixer_out, attn_out)


def solution(mesh):
    in_specs = (
        P(None, "ctx", "head"),
        P(None, "ctx", "head"),
        P(None, "ctx", "head"),
        P(None, "ctx", "head"),
        P(None, "ctx", "head"),
        P("head"),
        P("head"),
        P("head"),
        P("head", "ctx"),
        P(None, "ctx", "head"),
        P(None, "ctx", "head"),
        P(None, "ctx", "head"),
        P(None, "ctx"),
    )
    out_specs = (P(None, "ctx", "head"), P(None, "ctx", "head"))
    return jax.shard_map(shards, mesh=mesh, in_specs=in_specs, out_specs=out_specs, check_vma=False)
```

```python
import jax
import jax.numpy as jnp
import numpy as np
from jax import lax
from jax.sharding import PartitionSpec as P

P_SIZE = 64
N = 128
HD = 128
SPAN = 128


CTX = ("cyz", "core")
epsilon = 1e-05
lowest = -1e30


def shifted(value, axis, by):
    devices = lax.axis_size(axis)
    pairs = [(i, i + by) for i in range(devices) if 0 <= i + by < devices]
    return lax.ppermute(value, axis, pairs)


def link_states(earlier, later):
    decay_one, state_one, first_one, last_one = earlier
    decay_two, state_two, first_two, last_two = later
    passes = ((last_one == first_two) | (last_one < 0.0) | (first_two < 0.0)).astype(jnp.float32)
    through = passes[:, None] * decay_two
    decay = decay_one * through
    state = state_two + through[:, :, None, None] * state_one
    first = jnp.where(first_one < 0.0, first_two, first_one)
    last = jnp.where(last_two < 0.0, last_one, last_two)
    return (decay, state, first, last)


def shards(
    mixer_input,
    gate_input,
    state_in,
    state_out,
    step_sizes,
    decay_rates,
    skip_gain,
    norm_gain,
    out_weight,
    queries,
    keys,
    values,
    doc_ids,
):
    f32 = jnp.float32
    bf16 = jnp.bfloat16
    batches, length, channels = mixer_input.shape
    heads = step_sizes.shape[2]
    groups = state_in.shape[2] // N
    repeat = heads // groups
    count = length // SPAN
    reach = lax.axis_size(CTX) // 8
    position = lax.axis_index(CTX)
    core = lax.axis_index("core")

    width = keys.shape[2]
    doc_row = jnp.pad(doc_ids.astype(bf16), ((0, 0), (0, width)))[:, None, :]
    payload = jnp.concatenate([jnp.concatenate([keys, values], axis=2), doc_row], axis=1)
    arrivals = []
    for offset in range(reach, 0, -1):
        got = shifted(payload, CTX, offset)
        arrivals.append((got[:, :length, :width], got[:, :length, width:], got[:, length, :length]))

    x = mixer_input.reshape(batches, count, SPAN, heads, P_SIZE)
    dt = step_sizes.reshape(batches, count, SPAN, heads)
    docs = doc_ids.reshape(batches, count, SPAN)
    writers = state_in.reshape(batches, count, SPAN, groups, N)
    readers = state_out.reshape(batches, count, SPAN, groups, N)
    cum = jnp.cumsum(dt * decay_rates, axis=2)
    order = jnp.arange(SPAN, dtype=jnp.int32)
    causal = order[:, None] >= order[None, :]
    allowed = ((docs[:, :, :, None] == docs[:, :, None, :]) & causal)[:, :, None]
    cum_h = jnp.moveaxis(cum, 3, 2)
    spread = cum_h[..., :, None] - cum_h[..., None, :]
    decays = jnp.where(allowed, jnp.exp(-jnp.where(allowed, spread, 0.0)), 0.0)
    intersection = jnp.einsum(
        "bktgn,bksgn->bkgts", readers, writers, preferred_element_type=f32
    )
    intersection = jnp.repeat(intersection, repeat, axis=2)
    dt_h = jnp.moveaxis(dt, 3, 2)
    mixing = (decays * intersection * dt_h[:, :, :, None, :]).astype(bf16)
    within = jnp.einsum(
        "bkhts,bkshp->bkthp", mixing, x, preferred_element_type=f32
    )

    last_doc = docs[:, :, -1]
    ending = cum[:, :, -1:, :] - cum
    tailing = jnp.where((docs == last_doc[:, :, None])[..., None], jnp.exp(-ending), 0.0) * dt
    scaled = (tailing[..., None] * x.astype(f32)).astype(bf16)
    scaled = scaled.reshape(batches, count, SPAN, groups, repeat, P_SIZE)
    written = jnp.einsum(
        "bksgrp,bksgn->bkgrpn", scaled, writers, preferred_element_type=f32
    )
    totals = cum[:, :, -1, :]

    state = written[:, 0]
    block_outs = [within[:, 0]]
    for index in range(1, count):
        living = (docs[:, index] == last_doc[:, index - 1][:, None]).astype(f32)
        carried = jnp.einsum(
            "btgn,bgrpn->btgrp",
            readers[:, index],
            state.astype(bf16),
            preferred_element_type=f32,
        ).reshape(batches, SPAN, heads, P_SIZE)
        carried = carried * (jnp.exp(-cum[:, index]) * living[:, :, None])[..., None]
        block_outs.append(within[:, index] + carried)
        keeping = jnp.exp(-totals[:, index]) * (
            last_doc[:, index] == last_doc[:, index - 1]
        ).astype(f32)[:, None]
        state = state * keeping.reshape(batches, groups, repeat)[..., None, None] + written[:, index]
    local_out = jnp.stack(block_outs, axis=1).reshape(batches, length, heads, P_SIZE)

    cumulative = jnp.cumsum(step_sizes * decay_rates, axis=1)
    first_doc = doc_ids[:, 0]
    end_doc = doc_ids[:, -1]
    passing = jnp.exp(-cumulative[:, -1, :]) * (first_doc == end_doc).astype(f32)[:, None]
    own_state = state.reshape(batches, heads, P_SIZE, N)
    small = jnp.concatenate(
        [passing, first_doc.astype(f32)[:, None], end_doc.astype(f32)[:, None]], axis=1
    )
    small_row = jnp.pad(small, ((0, 0), (0, N - heads - 2)))[:, None, :]
    state_payload = jnp.concatenate(
        [own_state.reshape(batches, heads * P_SIZE, N), small_row], axis=1
    ).astype(bf16)
    received = []
    for offset in range(reach, 0, -1):
        got = shifted(state_payload, CTX, offset)
        got_small = got[:, heads * P_SIZE].astype(f32)
        got_state = got[:, : heads * P_SIZE].astype(f32).reshape(batches, heads, P_SIZE, N)
        received.append((got_small[:, :heads], got_state, got_small[:, heads], got_small[:, heads + 1]))
    before = received[0]
    for item in received[1:]:
        before = link_states(before, item)

    living = (doc_ids.astype(f32) == before[3][:, None]).astype(f32)
    carried = jnp.einsum(
        "btgn,bgrpn->btgrp",
        state_out.reshape(batches, length, groups, N),
        before[1].astype(bf16).reshape(batches, groups, repeat, P_SIZE, N),
        preferred_element_type=f32,
    ).reshape(batches, length, heads, P_SIZE)
    carried = carried * (jnp.exp(-cumulative) * living[:, :, None])[..., None]
    inputs = mixer_input.reshape(batches, length, heads, P_SIZE)
    mixed = local_out + carried + skip_gain[:, None] * inputs.astype(f32)
    gated = mixed.reshape(batches, length, channels) * jax.nn.silu(gate_input.astype(f32))
    shaped = gated.reshape(batches, length, groups, channels // groups)
    factor = lax.rsqrt(jnp.mean(shaped * shaped, axis=-1, keepdims=True) + epsilon)
    normed = ((shaped * factor).reshape(batches, length, channels) * norm_gain).astype(bf16)
    own_columns = lax.all_gather(out_weight, "cyz", axis=1, tiled=True)
    other_columns = lax.ppermute(own_columns, "core", [(0, 1), (1, 0)])
    column = out_weight.shape[1]
    blocks = own_columns.shape[1] // column
    first = jnp.einsum("btc,cd->btd", normed, own_columns, preferred_element_type=f32)
    second = jnp.einsum("btc,cd->btd", normed, other_columns, preferred_element_type=f32)
    projected = jnp.stack(
        [
            first.reshape(batches, length, blocks, column),
            second.reshape(batches, length, blocks, column),
        ],
        axis=3,
    ).reshape(batches, length, 2 * blocks * column)
    scattered = lax.psum_scatter(
        projected.astype(bf16), "head", scatter_dimension=2, tiled=True
    )
    pairs = scattered.reshape(batches, length, -1, 2, column)
    mixer_out = jnp.where(core == 0, pairs, pairs[:, :, :, ::-1]).reshape(scattered.shape)

    kv_heads = keys.shape[2] // HD
    q_repeat = queries.shape[2] // HD // kv_heads
    query_heads = queries.reshape(batches, length, kv_heads, q_repeat, HD)
    window_keys = jnp.concatenate([a[0] for a in arrivals] + [keys], axis=1)
    window_values = jnp.concatenate([a[1] for a in arrivals] + [values], axis=1)
    key_docs = []
    for index, item in enumerate(arrivals):
        offset = reach - index
        key_docs.append(jnp.where(position >= offset, item[2].astype(jnp.int32), -1))
    key_docs = jnp.concatenate(key_docs + [doc_ids], axis=1)
    window = (reach + 1) * length
    query_pos = reach * length + jnp.arange(length, dtype=jnp.int32)
    key_pos = jnp.arange(window, dtype=jnp.int32)
    key_heads = window_keys.reshape(batches, window, kv_heads, HD)
    value_heads = window_values.reshape(batches, window, kv_heads, HD)
    scale = HD ** (-0.5)
    scores = (
        jnp.einsum("bqgrd,bkgd->bgrqk", query_heads, key_heads, preferred_element_type=f32)
        * scale
    )
    allowed = (key_pos[None, :] <= query_pos[:, None])[None] & (
        key_docs[:, None, :] == doc_ids[:, :, None]
    )
    allowed = allowed[:, None, None]
    top = jnp.max(jnp.where(allowed, scores, lowest), axis=-1, keepdims=True)
    probs = jnp.where(allowed, jnp.exp(scores - top), 0.0)
    total = jnp.sum(probs, axis=-1)
    mixed_values = jnp.einsum(
        "bgrqk,bkgd->bgrqd", probs.astype(bf16), value_heads, preferred_element_type=f32
    )
    result = mixed_values / total[..., None]
    attn_out = (
        jnp.transpose(result, (0, 3, 1, 2, 4))
        .reshape(batches, length, kv_heads * q_repeat * HD)
        .astype(bf16)
    )
    return (mixer_out, attn_out)


def solution(mesh):
    devices = np.asarray(mesh.devices).reshape(-1, 2, mesh.shape["head"])
    mesh = jax.sharding.Mesh(devices, ("cyz", "core", "head"))
    in_specs = (
        P(None, CTX, "head"),
        P(None, CTX, "head"),
        P(None, CTX, "head"),
        P(None, CTX, "head"),
        P(None, CTX, "head"),
        P("head"),
        P("head"),
        P("head"),
        P("head", CTX),
        P(None, CTX, "head"),
        P(None, CTX, "head"),
        P(None, CTX, "head"),
        P(None, CTX),
    )
    out_specs = (P(None, CTX, "head"), P(None, CTX, "head"))
    return jax.shard_map(shards, mesh=mesh, in_specs=in_specs, out_specs=out_specs, check_vma=False)
```

```python
import jax
import jax.numpy as jnp
import numpy as np
from jax import lax
from jax.sharding import PartitionSpec as P

P_SIZE = 64
N = 128
HD = 128
SPAN = 128


CTX = ("cyz", "core")
epsilon = 1e-05
lowest = -1e30


def shifted(value, axis, by):
    devices = lax.axis_size(axis)
    pairs = [(i, i + by) for i in range(devices) if 0 <= i + by < devices]
    return lax.ppermute(value, axis, pairs)


def link_states(earlier, later):
    decay_one, state_one, first_one, last_one = earlier
    decay_two, state_two, first_two, last_two = later
    passes = ((last_one == first_two) | (last_one < 0.0) | (first_two < 0.0)).astype(jnp.float32)
    through = passes[:, None] * decay_two
    decay = decay_one * through
    state = state_two + through[:, :, None, None] * state_one
    first = jnp.where(first_one < 0.0, first_two, first_one)
    last = jnp.where(last_two < 0.0, last_one, last_two)
    return (decay, state, first, last)


def attention(queries, keys, values, arrivals, doc_ids, position, reach):
    f32 = jnp.float32
    bf16 = jnp.bfloat16
    batches, length = doc_ids.shape
    kv_heads = keys.shape[2] // HD
    q_repeat = queries.shape[2] // HD // kv_heads
    query_heads = queries.reshape(batches, length, kv_heads, q_repeat, HD)
    window_keys = jnp.concatenate([a[0] for a in arrivals] + [keys], axis=1)
    window_values = jnp.concatenate([a[1] for a in arrivals] + [values], axis=1)
    key_docs = []
    for index, item in enumerate(arrivals):
        offset = reach - index
        key_docs.append(jnp.where(position >= offset, item[2].astype(jnp.int32), -1))
    key_docs = jnp.concatenate(key_docs + [doc_ids], axis=1)
    window = (reach + 1) * length
    query_pos = reach * length + jnp.arange(length, dtype=jnp.int32)
    key_pos = jnp.arange(window, dtype=jnp.int32)
    key_heads = window_keys.reshape(batches, window, kv_heads, HD)
    value_heads = window_values.reshape(batches, window, kv_heads, HD)
    scale = HD ** (-0.5)
    scores = (
        jnp.einsum("bqgrd,bkgd->bgrqk", query_heads, key_heads, preferred_element_type=f32)
        * scale
    )
    allowed = (key_pos[None, :] <= query_pos[:, None])[None] & (
        key_docs[:, None, :] == doc_ids[:, :, None]
    )
    allowed = allowed[:, None, None]
    top = jnp.max(jnp.where(allowed, scores, lowest), axis=-1, keepdims=True)
    probs = jnp.where(allowed, jnp.exp(scores - top), 0.0)
    total = jnp.sum(probs, axis=-1)
    mixed_values = jnp.einsum(
        "bgrqk,bkgd->bgrqd", probs.astype(bf16), value_heads, preferred_element_type=f32
    )
    result = mixed_values / total[..., None]
    attn_out = (
        jnp.transpose(result, (0, 3, 1, 2, 4))
        .reshape(batches, length, kv_heads * q_repeat * HD)
        .astype(bf16)
    )
    return attn_out


def shards(
    mixer_input,
    gate_input,
    state_in,
    state_out,
    step_sizes,
    decay_rates,
    skip_gain,
    norm_gain,
    out_weight,
    queries,
    keys,
    values,
    doc_ids,
):
    f32 = jnp.float32
    bf16 = jnp.bfloat16
    batches, length, channels = mixer_input.shape
    heads = step_sizes.shape[2]
    groups = state_in.shape[2] // N
    repeat = heads // groups
    count = length // SPAN
    reach = lax.axis_size(CTX) // 8
    position = lax.axis_index(CTX)
    core = lax.axis_index("core")

    width = keys.shape[2]
    doc_row = jnp.pad(doc_ids.astype(bf16), ((0, 0), (0, width)))[:, None, :]
    payload = jnp.concatenate([jnp.concatenate([keys, values], axis=2), doc_row], axis=1)
    arrivals = []
    for offset in range(reach, 0, -1):
        got = shifted(payload, CTX, offset)
        arrivals.append((got[:, :length, :width], got[:, :length, width:], got[:, length, :length]))

    attn_out = attention(queries, keys, values, arrivals, doc_ids, position, reach)
    attn_out, mixer_input, gate_input, state_in, state_out, step_sizes = lax.optimization_barrier(
        (attn_out, mixer_input, gate_input, state_in, state_out, step_sizes)
    )

    x = mixer_input.reshape(batches, count, SPAN, heads, P_SIZE)
    dt = step_sizes.reshape(batches, count, SPAN, heads)
    docs = doc_ids.reshape(batches, count, SPAN)
    writers = state_in.reshape(batches, count, SPAN, groups, N)
    readers = state_out.reshape(batches, count, SPAN, groups, N)
    cum = jnp.cumsum(dt * decay_rates, axis=2)
    order = jnp.arange(SPAN, dtype=jnp.int32)
    causal = order[:, None] >= order[None, :]
    allowed = ((docs[:, :, :, None] == docs[:, :, None, :]) & causal)[:, :, None]
    cum_h = jnp.moveaxis(cum, 3, 2)
    spread = cum_h[..., :, None] - cum_h[..., None, :]
    decays = jnp.where(allowed, jnp.exp(-jnp.where(allowed, spread, 0.0)), 0.0)
    intersection = jnp.einsum(
        "bktgn,bksgn->bkgts", readers, writers, preferred_element_type=f32
    )
    intersection = jnp.repeat(intersection, repeat, axis=2)
    dt_h = jnp.moveaxis(dt, 3, 2)
    mixing = (decays * intersection * dt_h[:, :, :, None, :]).astype(bf16)
    within = jnp.einsum(
        "bkhts,bkshp->bkthp", mixing, x, preferred_element_type=f32
    )

    last_doc = docs[:, :, -1]
    ending = cum[:, :, -1:, :] - cum
    tailing = jnp.where((docs == last_doc[:, :, None])[..., None], jnp.exp(-ending), 0.0) * dt
    scaled = (tailing[..., None] * x.astype(f32)).astype(bf16)
    scaled = scaled.reshape(batches, count, SPAN, groups, repeat, P_SIZE)
    written = jnp.einsum(
        "bksgrp,bksgn->bkgrpn", scaled, writers, preferred_element_type=f32
    )
    totals = cum[:, :, -1, :]

    state = written[:, 0]
    block_outs = [within[:, 0]]
    for index in range(1, count):
        living = (docs[:, index] == last_doc[:, index - 1][:, None]).astype(f32)
        carried = jnp.einsum(
            "btgn,bgrpn->btgrp",
            readers[:, index],
            state.astype(bf16),
            preferred_element_type=f32,
        ).reshape(batches, SPAN, heads, P_SIZE)
        carried = carried * (jnp.exp(-cum[:, index]) * living[:, :, None])[..., None]
        block_outs.append(within[:, index] + carried)
        keeping = jnp.exp(-totals[:, index]) * (
            last_doc[:, index] == last_doc[:, index - 1]
        ).astype(f32)[:, None]
        state = state * keeping.reshape(batches, groups, repeat)[..., None, None] + written[:, index]
    local_out = jnp.stack(block_outs, axis=1).reshape(batches, length, heads, P_SIZE)

    cumulative = jnp.cumsum(step_sizes * decay_rates, axis=1)
    first_doc = doc_ids[:, 0]
    end_doc = doc_ids[:, -1]
    passing = jnp.exp(-cumulative[:, -1, :]) * (first_doc == end_doc).astype(f32)[:, None]
    own_state = state.reshape(batches, heads, P_SIZE, N)
    small = jnp.concatenate(
        [passing, first_doc.astype(f32)[:, None], end_doc.astype(f32)[:, None]], axis=1
    )
    small_row = jnp.pad(small, ((0, 0), (0, N - heads - 2)))[:, None, :]
    state_payload = jnp.concatenate(
        [own_state.reshape(batches, heads * P_SIZE, N), small_row], axis=1
    ).astype(bf16)
    received = []
    for offset in range(reach, 0, -1):
        got = shifted(state_payload, CTX, offset)
        got_small = got[:, heads * P_SIZE].astype(f32)
        got_state = got[:, : heads * P_SIZE].astype(f32).reshape(batches, heads, P_SIZE, N)
        received.append((got_small[:, :heads], got_state, got_small[:, heads], got_small[:, heads + 1]))
    before = received[0]
    for item in received[1:]:
        before = link_states(before, item)

    living = (doc_ids.astype(f32) == before[3][:, None]).astype(f32)
    carried = jnp.einsum(
        "btgn,bgrpn->btgrp",
        state_out.reshape(batches, length, groups, N),
        before[1].astype(bf16).reshape(batches, groups, repeat, P_SIZE, N),
        preferred_element_type=f32,
    ).reshape(batches, length, heads, P_SIZE)
    carried = carried * (jnp.exp(-cumulative) * living[:, :, None])[..., None]
    inputs = mixer_input.reshape(batches, length, heads, P_SIZE)
    mixed = local_out + carried + skip_gain[:, None] * inputs.astype(f32)
    gated = mixed.reshape(batches, length, channels) * jax.nn.silu(gate_input.astype(f32))
    shaped = gated.reshape(batches, length, groups, channels // groups)
    factor = lax.rsqrt(jnp.mean(shaped * shaped, axis=-1, keepdims=True) + epsilon)
    normed = ((shaped * factor).reshape(batches, length, channels) * norm_gain).astype(bf16)
    projected = jnp.einsum(
        "btc,cd->btd",
        normed,
        lax.all_gather(out_weight, CTX, axis=1, tiled=True),
        preferred_element_type=f32,
    ).astype(bf16)
    parts = lax.axis_size("head")
    me = lax.axis_index("head")
    pieces = projected.reshape(batches, length, parts, -1)
    summed = lax.dynamic_index_in_dim(pieces, me, axis=2, keepdims=False).astype(f32)
    for offset in range(1, parts):
        target = (me + offset) % parts
        piece = lax.dynamic_index_in_dim(pieces, target, axis=2, keepdims=False)
        pairs = [(i, (i + offset) % parts) for i in range(parts)]
        summed = summed + lax.ppermute(piece, "head", pairs).astype(f32)
    mixer_out = summed.astype(bf16)

    return (mixer_out, attn_out)


def solution(mesh):
    devices = np.asarray(mesh.devices).reshape(-1, 2, mesh.shape["head"])
    mesh = jax.sharding.Mesh(devices, ("cyz", "core", "head"))
    in_specs = (
        P(None, CTX, "head"),
        P(None, CTX, "head"),
        P(None, CTX, "head"),
        P(None, CTX, "head"),
        P(None, CTX, "head"),
        P("head"),
        P("head"),
        P("head"),
        P("head", CTX),
        P(None, CTX, "head"),
        P(None, CTX, "head"),
        P(None, CTX, "head"),
        P(None, CTX),
    )
    out_specs = (P(None, CTX, "head"), P(None, CTX, "head"))
    return jax.shard_map(shards, mesh=mesh, in_specs=in_specs, out_specs=out_specs, check_vma=False)
```

```python
import jax
import jax.numpy as jnp
from jax import lax
from jax.sharding import PartitionSpec as P

P_SIZE = 64
N = 128
HD = 128
SPAN = 128


epsilon = 1e-05
lowest = -1e30


def shifted(value, axis, by):
    devices = lax.axis_size(axis)
    pairs = [(i, i + by) for i in range(devices) if 0 <= i + by < devices]
    return lax.ppermute(value, axis, pairs)


def link_states(earlier, later):
    decay_one, state_one, first_one, last_one = earlier
    decay_two, state_two, first_two, last_two = later
    passes = ((last_one == first_two) | (last_one < 0.0) | (first_two < 0.0)).astype(jnp.float32)
    through = passes[:, None] * decay_two
    decay = decay_one * through
    state = state_two + through[:, :, None, None] * state_one
    first = jnp.where(first_one < 0.0, first_two, first_one)
    last = jnp.where(last_two < 0.0, last_one, last_two)
    return (decay, state, first, last)


def shards(
    mixer_input,
    gate_input,
    state_in,
    state_out,
    step_sizes,
    decay_rates,
    skip_gain,
    norm_gain,
    out_weight,
    queries,
    keys,
    values,
    doc_ids,
):
    f32 = jnp.float32
    bf16 = jnp.bfloat16
    batches, length, channels = mixer_input.shape
    heads = step_sizes.shape[2]
    groups = state_in.shape[2] // N
    repeat = heads // groups
    count = length // SPAN
    reach = lax.axis_size("ctx") // 8
    position = lax.axis_index("ctx")

    width = keys.shape[2]
    doc_row = jnp.pad(doc_ids.astype(bf16), ((0, 0), (0, width)))[:, None, :]
    payload = jnp.concatenate([jnp.concatenate([keys, values], axis=2), doc_row], axis=1)
    arrivals = []
    for offset in range(reach, 0, -1):
        arrivals.append(shifted(payload, "ctx", offset))

    x = mixer_input.reshape(batches, count, SPAN, heads, P_SIZE)
    dt = step_sizes.reshape(batches, count, SPAN, heads)
    docs = doc_ids.reshape(batches, count, SPAN)
    writers = state_in.reshape(batches, count, SPAN, groups, N)
    readers = state_out.reshape(batches, count, SPAN, groups, N)
    cum = jnp.cumsum(dt * decay_rates, axis=2)
    order = jnp.arange(SPAN, dtype=jnp.int32)
    causal = order[:, None] >= order[None, :]
    allowed = ((docs[:, :, :, None] == docs[:, :, None, :]) & causal)[:, :, None]
    cum_h = jnp.moveaxis(cum, 3, 2)
    spread = cum_h[..., :, None] - cum_h[..., None, :]
    decays = jnp.where(allowed, jnp.exp(-jnp.where(allowed, spread, 0.0)), 0.0)
    intersection = jnp.einsum(
        "bktgn,bksgn->bkgts", readers, writers, preferred_element_type=f32
    )
    intersection = jnp.repeat(intersection, repeat, axis=2)
    dt_h = jnp.moveaxis(dt, 3, 2)
    mixing = (decays * intersection * dt_h[:, :, :, None, :]).astype(bf16)
    within = jnp.einsum(
        "bkhts,bkshp->bkthp", mixing, x, preferred_element_type=f32
    )
    arrivals, within = lax.optimization_barrier((arrivals, within))
    arrivals = [
        (got[:, :length, :width], got[:, :length, width:], got[:, length, :length]) for got in arrivals
    ]

    last_doc = docs[:, :, -1]
    ending = cum[:, :, -1:, :] - cum
    tailing = jnp.where((docs == last_doc[:, :, None])[..., None], jnp.exp(-ending), 0.0) * dt
    scaled = (tailing[..., None] * x.astype(f32)).astype(bf16)
    scaled = scaled.reshape(batches, count, SPAN, groups, repeat, P_SIZE)
    written = jnp.einsum(
        "bksgrp,bksgn->bkgrpn", scaled, writers, preferred_element_type=f32
    )
    totals = cum[:, :, -1, :]

    state = written[:, 0]
    block_outs = [within[:, 0]]
    for index in range(1, count):
        living = (docs[:, index] == last_doc[:, index - 1][:, None]).astype(f32)
        carried = jnp.einsum(
            "btgn,bgrpn->btgrp",
            readers[:, index],
            state.astype(bf16),
            preferred_element_type=f32,
        ).reshape(batches, SPAN, heads, P_SIZE)
        carried = carried * (jnp.exp(-cum[:, index]) * living[:, :, None])[..., None]
        block_outs.append(within[:, index] + carried)
        keeping = jnp.exp(-totals[:, index]) * (
            last_doc[:, index] == last_doc[:, index - 1]
        ).astype(f32)[:, None]
        state = state * keeping.reshape(batches, groups, repeat)[..., None, None] + written[:, index]
    local_out = jnp.stack(block_outs, axis=1).reshape(batches, length, heads, P_SIZE)

    cumulative = jnp.cumsum(step_sizes * decay_rates, axis=1)
    first_doc = doc_ids[:, 0]
    end_doc = doc_ids[:, -1]
    passing = jnp.exp(-cumulative[:, -1, :]) * (first_doc == end_doc).astype(f32)[:, None]
    own_state = state.reshape(batches, heads, P_SIZE, N)
    small = jnp.concatenate(
        [passing, first_doc.astype(f32)[:, None], end_doc.astype(f32)[:, None]], axis=1
    )
    received = []
    for offset in range(reach, 0, -1):
        got_small, got_state = shifted((small, own_state.astype(bf16)), "ctx", offset)
        received.append(
            (got_small[:, :heads], got_state.astype(f32), got_small[:, heads], got_small[:, heads + 1])
        )
    before = received[0]
    for item in received[1:]:
        before = link_states(before, item)

    living = (doc_ids.astype(f32) == before[3][:, None]).astype(f32)
    carried = jnp.einsum(
        "btgn,bgrpn->btgrp",
        state_out.reshape(batches, length, groups, N),
        before[1].astype(bf16).reshape(batches, groups, repeat, P_SIZE, N),
        preferred_element_type=f32,
    ).reshape(batches, length, heads, P_SIZE)
    carried = carried * (jnp.exp(-cumulative) * living[:, :, None])[..., None]
    inputs = mixer_input.reshape(batches, length, heads, P_SIZE)
    mixed = local_out + carried + skip_gain[:, None] * inputs.astype(f32)
    gated = mixed.reshape(batches, length, channels) * jax.nn.silu(gate_input.astype(f32))
    shaped = gated.reshape(batches, length, groups, channels // groups)
    factor = lax.rsqrt(jnp.mean(shaped * shaped, axis=-1, keepdims=True) + epsilon)
    normed = ((shaped * factor).reshape(batches, length, channels) * norm_gain).astype(bf16)
    projected = jnp.einsum(
        "btc,cd->btd",
        normed,
        lax.all_gather(out_weight, "ctx", axis=1, tiled=True),
        preferred_element_type=f32,
    )
    mixer_out = lax.psum_scatter(
        projected.astype(bf16), "head", scatter_dimension=2, tiled=True
    )

    kv_heads = keys.shape[2] // HD
    q_repeat = queries.shape[2] // HD // kv_heads
    query_heads = queries.reshape(batches, length, kv_heads, q_repeat, HD)
    window_keys = jnp.concatenate([a[0] for a in arrivals] + [keys], axis=1)
    window_values = jnp.concatenate([a[1] for a in arrivals] + [values], axis=1)
    key_docs = []
    for index, item in enumerate(arrivals):
        offset = reach - index
        key_docs.append(jnp.where(position >= offset, item[2].astype(jnp.int32), -1))
    key_docs = jnp.concatenate(key_docs + [doc_ids], axis=1)
    window = (reach + 1) * length
    query_pos = reach * length + jnp.arange(length, dtype=jnp.int32)
    key_pos = jnp.arange(window, dtype=jnp.int32)
    key_heads = window_keys.reshape(batches, window, kv_heads, HD)
    value_heads = window_values.reshape(batches, window, kv_heads, HD)
    scale = HD ** (-0.5)
    scores = (
        jnp.einsum("bqgrd,bkgd->bgrqk", query_heads, key_heads, preferred_element_type=f32)
        * scale
    )
    allowed = (key_pos[None, :] <= query_pos[:, None])[None] & (
        key_docs[:, None, :] == doc_ids[:, :, None]
    )
    allowed = allowed[:, None, None]
    top = jnp.max(jnp.where(allowed, scores, lowest), axis=-1, keepdims=True)
    probs = jnp.where(allowed, jnp.exp(scores - top), 0.0)
    total = jnp.sum(probs, axis=-1)
    mixed_values = jnp.einsum(
        "bgrqk,bkgd->bgrqd", probs.astype(bf16), value_heads, preferred_element_type=f32
    )
    result = mixed_values / total[..., None]
    attn_out = (
        jnp.transpose(result, (0, 3, 1, 2, 4))
        .reshape(batches, length, kv_heads * q_repeat * HD)
        .astype(bf16)
    )
    return (mixer_out, attn_out)


def solution(mesh):
    in_specs = (
        P(None, "ctx", "head"),
        P(None, "ctx", "head"),
        P(None, "ctx", "head"),
        P(None, "ctx", "head"),
        P(None, "ctx", "head"),
        P("head"),
        P("head"),
        P("head"),
        P("head", "ctx"),
        P(None, "ctx", "head"),
        P(None, "ctx", "head"),
        P(None, "ctx", "head"),
        P(None, "ctx"),
    )
    out_specs = (P(None, "ctx", "head"), P(None, "ctx", "head"))
    return jax.shard_map(shards, mesh=mesh, in_specs=in_specs, out_specs=out_specs, check_vma=False)
```

```python
import jax
import jax.numpy as jnp
from jax import lax
from jax.sharding import PartitionSpec as P

P_SIZE = 64
N = 128
HD = 128
SPAN = 128


epsilon = 1e-05
lowest = -1e30


def shifted(value, axis, by):
    devices = lax.axis_size(axis)
    pairs = [(i, i + by) for i in range(devices) if 0 <= i + by < devices]
    return lax.ppermute(value, axis, pairs)


def link_states(earlier, later):
    decay_one, state_one, first_one, last_one = earlier
    decay_two, state_two, first_two, last_two = later
    passes = ((last_one == first_two) | (last_one < 0.0) | (first_two < 0.0)).astype(jnp.float32)
    through = passes[:, None] * decay_two
    decay = decay_one * through
    state = state_two + through[:, :, None, None] * state_one
    first = jnp.where(first_one < 0.0, first_two, first_one)
    last = jnp.where(last_two < 0.0, last_one, last_two)
    return (decay, state, first, last)


def shards(
    mixer_input,
    gate_input,
    state_in,
    state_out,
    step_sizes,
    decay_rates,
    skip_gain,
    norm_gain,
    out_weight,
    queries,
    keys,
    values,
    doc_ids,
):
    f32 = jnp.float32
    bf16 = jnp.bfloat16
    batches, length, channels = mixer_input.shape
    heads = step_sizes.shape[2]
    groups = state_in.shape[2] // N
    repeat = heads // groups
    count = length // SPAN
    reach = lax.axis_size("ctx") // 8
    position = lax.axis_index("ctx")

    width = keys.shape[2]
    doc_row = jnp.pad(doc_ids.astype(bf16), ((0, 0), (0, width)))[:, None, :]
    payload = jnp.concatenate([jnp.concatenate([keys, values], axis=2), doc_row], axis=1)
    arrivals = []
    for offset in range(reach, 0, -1):
        arrivals.append(shifted(payload, "ctx", offset))

    x = mixer_input.reshape(batches, count, SPAN, heads, P_SIZE)
    dt = step_sizes.reshape(batches, count, SPAN, heads)
    docs = doc_ids.reshape(batches, count, SPAN)
    writers = state_in.reshape(batches, count, SPAN, groups, N)
    readers = state_out.reshape(batches, count, SPAN, groups, N)
    cum = jnp.cumsum(dt * decay_rates, axis=2)
    order = jnp.arange(SPAN, dtype=jnp.int32)
    causal = order[:, None] >= order[None, :]
    allowed = ((docs[:, :, :, None] == docs[:, :, None, :]) & causal)[:, :, None]
    cum_h = jnp.moveaxis(cum, 3, 2)
    spread = cum_h[..., :, None] - cum_h[..., None, :]
    decays = jnp.where(allowed, jnp.exp(-jnp.where(allowed, spread, 0.0)), 0.0)
    intersection = jnp.einsum(
        "bktgn,bksgn->bkgts", readers, writers, preferred_element_type=f32
    )
    intersection = jnp.repeat(intersection, repeat, axis=2)
    dt_h = jnp.moveaxis(dt, 3, 2)
    mixing = (decays * intersection * dt_h[:, :, :, None, :]).astype(bf16)
    within = jnp.einsum(
        "bkhts,bkshp->bkthp", mixing, x, preferred_element_type=f32
    )
    arrivals, within = lax.optimization_barrier((arrivals, within))
    arrivals = [
        (got[:, :length, :width], got[:, :length, width:], got[:, length, :length]) for got in arrivals
    ]

    last_doc = docs[:, :, -1]
    ending = cum[:, :, -1:, :] - cum
    tailing = jnp.where((docs == last_doc[:, :, None])[..., None], jnp.exp(-ending), 0.0) * dt
    scaled = (tailing[..., None] * x.astype(f32)).astype(bf16)
    scaled = scaled.reshape(batches, count, SPAN, groups, repeat, P_SIZE)
    written = jnp.einsum(
        "bksgrp,bksgn->bkgrpn", scaled, writers, preferred_element_type=f32
    )
    totals = cum[:, :, -1, :]

    state = written[:, 0]
    block_outs = [within[:, 0]]
    for index in range(1, count):
        living = (docs[:, index] == last_doc[:, index - 1][:, None]).astype(f32)
        carried = jnp.einsum(
            "btgn,bgrpn->btgrp",
            readers[:, index],
            state.astype(bf16),
            preferred_element_type=f32,
        ).reshape(batches, SPAN, heads, P_SIZE)
        carried = carried * (jnp.exp(-cum[:, index]) * living[:, :, None])[..., None]
        block_outs.append(within[:, index] + carried)
        keeping = jnp.exp(-totals[:, index]) * (
            last_doc[:, index] == last_doc[:, index - 1]
        ).astype(f32)[:, None]
        state = state * keeping.reshape(batches, groups, repeat)[..., None, None] + written[:, index]
    local_out = jnp.stack(block_outs, axis=1).reshape(batches, length, heads, P_SIZE)

    cumulative = jnp.cumsum(step_sizes * decay_rates, axis=1)
    first_doc = doc_ids[:, 0]
    end_doc = doc_ids[:, -1]
    passing = jnp.exp(-cumulative[:, -1, :]) * (first_doc == end_doc).astype(f32)[:, None]
    own_state = state.reshape(batches, heads, P_SIZE, N)
    small = jnp.concatenate(
        [passing, first_doc.astype(f32)[:, None], end_doc.astype(f32)[:, None]], axis=1
    )
    received = []
    for offset in range(reach, 0, -1):
        got_small, got_state = shifted((small, own_state.astype(bf16)), "ctx", offset)
        received.append(
            (got_small[:, :heads], got_state.astype(f32), got_small[:, heads], got_small[:, heads + 1])
        )
    before = received[0]
    for item in received[1:]:
        before = link_states(before, item)

    living = (doc_ids.astype(f32) == before[3][:, None]).astype(f32)
    carried = jnp.einsum(
        "btgn,bgrpn->btgrp",
        state_out.reshape(batches, length, groups, N),
        before[1].astype(bf16).reshape(batches, groups, repeat, P_SIZE, N),
        preferred_element_type=f32,
    ).reshape(batches, length, heads, P_SIZE)
    carried = carried * (jnp.exp(-cumulative) * living[:, :, None])[..., None]
    inputs = mixer_input.reshape(batches, length, heads, P_SIZE)
    mixed = local_out + carried + skip_gain[:, None] * inputs.astype(f32)
    gated = mixed.reshape(batches, length, channels) * jax.nn.silu(gate_input.astype(f32))
    shaped = gated.reshape(batches, length, groups, channels // groups)
    factor = lax.rsqrt(jnp.mean(shaped * shaped, axis=-1, keepdims=True) + epsilon)
    normed = ((shaped * factor).reshape(batches, length, channels) * norm_gain).astype(bf16)
    projected = jnp.einsum(
        "btc,cd->btd",
        normed,
        lax.all_gather(out_weight, "ctx", axis=1, tiled=True),
        preferred_element_type=f32,
    )
    parts = lax.axis_size("head")
    pieces = projected.astype(bf16).reshape(batches, length, parts, -1)
    pieces = lax.all_to_all(pieces, "head", 2, 2, tiled=True)
    mixer_out = jnp.sum(pieces.astype(f32), axis=2).astype(bf16)

    kv_heads = keys.shape[2] // HD
    q_repeat = queries.shape[2] // HD // kv_heads
    query_heads = queries.reshape(batches, length, kv_heads, q_repeat, HD)
    window_keys = jnp.concatenate([a[0] for a in arrivals] + [keys], axis=1)
    window_values = jnp.concatenate([a[1] for a in arrivals] + [values], axis=1)
    key_docs = []
    for index, item in enumerate(arrivals):
        offset = reach - index
        key_docs.append(jnp.where(position >= offset, item[2].astype(jnp.int32), -1))
    key_docs = jnp.concatenate(key_docs + [doc_ids], axis=1)
    window = (reach + 1) * length
    query_pos = reach * length + jnp.arange(length, dtype=jnp.int32)
    key_pos = jnp.arange(window, dtype=jnp.int32)
    key_heads = window_keys.reshape(batches, window, kv_heads, HD)
    value_heads = window_values.reshape(batches, window, kv_heads, HD)
    scale = HD ** (-0.5)
    scores = (
        jnp.einsum("bqgrd,bkgd->bgrqk", query_heads, key_heads, preferred_element_type=f32)
        * scale
    )
    allowed = (key_pos[None, :] <= query_pos[:, None])[None] & (
        key_docs[:, None, :] == doc_ids[:, :, None]
    )
    allowed = allowed[:, None, None]
    top = jnp.max(jnp.where(allowed, scores, lowest), axis=-1, keepdims=True)
    probs = jnp.where(allowed, jnp.exp(scores - top), 0.0)
    total = jnp.sum(probs, axis=-1)
    mixed_values = jnp.einsum(
        "bgrqk,bkgd->bgrqd", probs.astype(bf16), value_heads, preferred_element_type=f32
    )
    result = mixed_values / total[..., None]
    attn_out = (
        jnp.transpose(result, (0, 3, 1, 2, 4))
        .reshape(batches, length, kv_heads * q_repeat * HD)
        .astype(bf16)
    )
    return (mixer_out, attn_out)


def solution(mesh):
    in_specs = (
        P(None, "ctx", "head"),
        P(None, "ctx", "head"),
        P(None, "ctx", "head"),
        P(None, "ctx", "head"),
        P(None, "ctx", "head"),
        P("head"),
        P("head"),
        P("head"),
        P("head", "ctx"),
        P(None, "ctx", "head"),
        P(None, "ctx", "head"),
        P(None, "ctx", "head"),
        P(None, "ctx"),
    )
    out_specs = (P(None, "ctx", "head"), P(None, "ctx", "head"))
    return jax.shard_map(shards, mesh=mesh, in_specs=in_specs, out_specs=out_specs, check_vma=False)
```

```python
import jax
import jax.numpy as jnp
from jax import lax
from jax.sharding import PartitionSpec as P

P_SIZE = 64
N = 128
HD = 128
SPAN = 128


epsilon = 1e-05
lowest = -1e30


def shifted(value, axis, by):
    devices = lax.axis_size(axis)
    pairs = [(i, i + by) for i in range(devices) if 0 <= i + by < devices]
    return lax.ppermute(value, axis, pairs)


def link_states(earlier, later):
    decay_one, state_one, first_one, last_one = earlier
    decay_two, state_two, first_two, last_two = later
    passes = ((last_one == first_two) | (last_one < 0.0) | (first_two < 0.0)).astype(jnp.float32)
    through = passes[:, None] * decay_two
    decay = decay_one * through
    state = state_two + through[:, :, None, None] * state_one
    first = jnp.where(first_one < 0.0, first_two, first_one)
    last = jnp.where(last_two < 0.0, last_one, last_two)
    return (decay, state, first, last)


def shards(
    mixer_input,
    gate_input,
    state_in,
    state_out,
    step_sizes,
    decay_rates,
    skip_gain,
    norm_gain,
    out_weight,
    queries,
    keys,
    values,
    doc_ids,
):
    f32 = jnp.float32
    bf16 = jnp.bfloat16
    batches, length, channels = mixer_input.shape
    heads = step_sizes.shape[2]
    groups = state_in.shape[2] // N
    repeat = heads // groups
    count = length // SPAN
    reach = lax.axis_size("ctx") // 8
    position = lax.axis_index("ctx")

    doc_send = doc_ids.astype(bf16)
    arrivals = []
    for offset in range(reach, 0, -1):
        arrivals.append(shifted((keys, values, doc_send), "ctx", offset))

    x = mixer_input.reshape(batches, count, SPAN, heads, P_SIZE)
    dt = step_sizes.reshape(batches, count, SPAN, heads)
    docs = doc_ids.reshape(batches, count, SPAN)
    writers = state_in.reshape(batches, count, SPAN, groups, N)
    readers = state_out.reshape(batches, count, SPAN, groups, N)
    cum = jnp.cumsum(dt * decay_rates, axis=2)
    order = jnp.arange(SPAN, dtype=jnp.int32)
    causal = order[:, None] >= order[None, :]
    allowed = ((docs[:, :, :, None] == docs[:, :, None, :]) & causal)[:, :, None]
    cum_h = jnp.moveaxis(cum, 3, 2)
    spread = cum_h[..., :, None] - cum_h[..., None, :]
    decays = jnp.where(allowed, jnp.exp(-jnp.where(allowed, spread, 0.0)), 0.0)
    intersection = jnp.einsum(
        "bktgn,bksgn->bkgts", readers, writers, preferred_element_type=f32
    )
    intersection = jnp.repeat(intersection, repeat, axis=2)
    dt_h = jnp.moveaxis(dt, 3, 2)
    mixing = (decays * intersection * dt_h[:, :, :, None, :]).astype(bf16)
    within = jnp.einsum(
        "bkhts,bkshp->bkthp", mixing, x, preferred_element_type=f32
    )

    last_doc = docs[:, :, -1]
    ending = cum[:, :, -1:, :] - cum
    tailing = jnp.where((docs == last_doc[:, :, None])[..., None], jnp.exp(-ending), 0.0) * dt
    scaled = (tailing[..., None] * x.astype(f32)).astype(bf16)
    scaled = scaled.reshape(batches, count, SPAN, groups, repeat, P_SIZE)
    written = jnp.einsum(
        "bksgrp,bksgn->bkgrpn", scaled, writers, preferred_element_type=f32
    )
    totals = cum[:, :, -1, :]

    state = written[:, 0]
    block_outs = [within[:, 0]]
    for index in range(1, count):
        living = (docs[:, index] == last_doc[:, index - 1][:, None]).astype(f32)
        carried = jnp.einsum(
            "btgn,bgrpn->btgrp",
            readers[:, index],
            state.astype(bf16),
            preferred_element_type=f32,
        ).reshape(batches, SPAN, heads, P_SIZE)
        carried = carried * (jnp.exp(-cum[:, index]) * living[:, :, None])[..., None]
        block_outs.append(within[:, index] + carried)
        keeping = jnp.exp(-totals[:, index]) * (
            last_doc[:, index] == last_doc[:, index - 1]
        ).astype(f32)[:, None]
        state = state * keeping.reshape(batches, groups, repeat)[..., None, None] + written[:, index]
    local_out = jnp.stack(block_outs, axis=1).reshape(batches, length, heads, P_SIZE)

    cumulative = jnp.cumsum(step_sizes * decay_rates, axis=1)
    first_doc = doc_ids[:, 0]
    end_doc = doc_ids[:, -1]
    passing = jnp.exp(-cumulative[:, -1, :]) * (first_doc == end_doc).astype(f32)[:, None]
    own_state = state.reshape(batches, heads, P_SIZE, N)
    small = jnp.concatenate(
        [passing, first_doc.astype(f32)[:, None], end_doc.astype(f32)[:, None]], axis=1
    )
    def send(summary, by):
        tiny = jnp.concatenate([summary[0], summary[2][:, None], summary[3][:, None]], axis=1)
        got_small, got_state = shifted((tiny, summary[1].astype(bf16)), "ctx", by)
        return (got_small[:, :heads], got_state.astype(f32), got_small[:, heads], got_small[:, heads + 1])

    own = (passing, own_state, first_doc.astype(f32), end_doc.astype(f32))
    one_back = send(own, 1)
    two_back = send(own, 2)
    three_to_here = link_states(link_states(two_back, one_back), own)
    before = link_states(send(three_to_here, 2), one_back)

    living = (doc_ids.astype(f32) == before[3][:, None]).astype(f32)
    carried = jnp.einsum(
        "btgn,bgrpn->btgrp",
        state_out.reshape(batches, length, groups, N),
        before[1].astype(bf16).reshape(batches, groups, repeat, P_SIZE, N),
        preferred_element_type=f32,
    ).reshape(batches, length, heads, P_SIZE)
    carried = carried * (jnp.exp(-cumulative) * living[:, :, None])[..., None]
    inputs = mixer_input.reshape(batches, length, heads, P_SIZE)
    mixed = local_out + carried + skip_gain[:, None] * inputs.astype(f32)
    gated = mixed.reshape(batches, length, channels) * jax.nn.silu(gate_input.astype(f32))
    shaped = gated.reshape(batches, length, groups, channels // groups)
    factor = lax.rsqrt(jnp.mean(shaped * shaped, axis=-1, keepdims=True) + epsilon)
    normed = ((shaped * factor).reshape(batches, length, channels) * norm_gain).astype(bf16)
    projected = jnp.einsum(
        "btc,cd->btd",
        normed,
        lax.all_gather(out_weight, "ctx", axis=1, tiled=True),
        preferred_element_type=f32,
    )
    mixer_out = lax.psum_scatter(
        projected.astype(bf16), "head", scatter_dimension=2, tiled=True
    )

    kv_heads = keys.shape[2] // HD
    q_repeat = queries.shape[2] // HD // kv_heads
    query_heads = queries.reshape(batches, length, kv_heads, q_repeat, HD)
    window_keys = jnp.concatenate([a[0] for a in arrivals] + [keys], axis=1)
    window_values = jnp.concatenate([a[1] for a in arrivals] + [values], axis=1)
    key_docs = []
    for index, item in enumerate(arrivals):
        offset = reach - index
        key_docs.append(jnp.where(position >= offset, item[2].astype(jnp.int32), -1))
    key_docs = jnp.concatenate(key_docs + [doc_ids], axis=1)
    window = (reach + 1) * length
    query_pos = reach * length + jnp.arange(length, dtype=jnp.int32)
    key_pos = jnp.arange(window, dtype=jnp.int32)
    key_heads = window_keys.reshape(batches, window, kv_heads, HD)
    value_heads = window_values.reshape(batches, window, kv_heads, HD)
    scale = HD ** (-0.5)
    scores = (
        jnp.einsum("bqgrd,bkgd->bgrqk", query_heads, key_heads, preferred_element_type=f32)
        * scale
    )
    allowed = (key_pos[None, :] <= query_pos[:, None])[None] & (
        key_docs[:, None, :] == doc_ids[:, :, None]
    )
    allowed = allowed[:, None, None]
    top = jnp.max(jnp.where(allowed, scores, lowest), axis=-1, keepdims=True)
    probs = jnp.where(allowed, jnp.exp(scores - top), 0.0)
    total = jnp.sum(probs, axis=-1)
    mixed_values = jnp.einsum(
        "bgrqk,bkgd->bgrqd", probs.astype(bf16), value_heads, preferred_element_type=f32
    )
    result = mixed_values / total[..., None]
    attn_out = (
        jnp.transpose(result, (0, 3, 1, 2, 4))
        .reshape(batches, length, kv_heads * q_repeat * HD)
        .astype(bf16)
    )
    return (mixer_out, attn_out)


def solution(mesh):
    in_specs = (
        P(None, "ctx", "head"),
        P(None, "ctx", "head"),
        P(None, "ctx", "head"),
        P(None, "ctx", "head"),
        P(None, "ctx", "head"),
        P("head"),
        P("head"),
        P("head"),
        P("head", "ctx"),
        P(None, "ctx", "head"),
        P(None, "ctx", "head"),
        P(None, "ctx", "head"),
        P(None, "ctx"),
    )
    out_specs = (P(None, "ctx", "head"), P(None, "ctx", "head"))
    return jax.shard_map(shards, mesh=mesh, in_specs=in_specs, out_specs=out_specs, check_vma=False)
```

```python
import jax
import jax.numpy as jnp
from jax import lax
from jax.sharding import PartitionSpec as P

P_SIZE = 64
N = 128
HD = 128
SPAN = 128


epsilon = 1e-05
lowest = -1e30


def shifted(value, axis, by):
    devices = lax.axis_size(axis)
    pairs = [(i, i + by) for i in range(devices) if 0 <= i + by < devices]
    return lax.ppermute(value, axis, pairs)


def link_states(earlier, later):
    decay_one, state_one, first_one, last_one = earlier
    decay_two, state_two, first_two, last_two = later
    passes = ((last_one == first_two) | (last_one < 0.0) | (first_two < 0.0)).astype(jnp.float32)
    through = passes[:, None] * decay_two
    decay = decay_one * through
    state = state_two + through[:, :, None, None] * state_one
    first = jnp.where(first_one < 0.0, first_two, first_one)
    last = jnp.where(last_two < 0.0, last_one, last_two)
    return (decay, state, first, last)


def shards(
    mixer_input,
    gate_input,
    state_in,
    state_out,
    step_sizes,
    decay_rates,
    skip_gain,
    norm_gain,
    out_weight,
    queries,
    keys,
    values,
    doc_ids,
):
    f32 = jnp.float32
    bf16 = jnp.bfloat16
    batches, length, channels = mixer_input.shape
    heads = step_sizes.shape[2]
    groups = state_in.shape[2] // N
    repeat = heads // groups
    count = length // SPAN
    reach = lax.axis_size("ctx") // 8
    position = lax.axis_index("ctx")

    width = keys.shape[2]
    doc_row = jnp.pad(doc_ids.astype(bf16), ((0, 0), (0, width)))[:, None, :]
    payload = jnp.concatenate([jnp.concatenate([keys, values], axis=2), doc_row], axis=1)
    arrivals = []
    for offset in range(reach, 0, -1):
        got = shifted(payload, "ctx", offset)
        arrivals.append((got[:, :length, :width], got[:, :length, width:], got[:, length, :length]))

    x = mixer_input.reshape(batches, count, SPAN, heads, P_SIZE)
    dt = step_sizes.reshape(batches, count, SPAN, heads)
    docs = doc_ids.reshape(batches, count, SPAN)
    writers = state_in.reshape(batches, count, SPAN, groups, N)
    readers = state_out.reshape(batches, count, SPAN, groups, N)
    cum = jnp.cumsum(dt * decay_rates, axis=2)
    order = jnp.arange(SPAN, dtype=jnp.int32)
    causal = order[:, None] >= order[None, :]
    allowed = ((docs[:, :, :, None] == docs[:, :, None, :]) & causal)[:, :, None]
    cum_h = jnp.moveaxis(cum, 3, 2)
    spread = cum_h[..., :, None] - cum_h[..., None, :]
    decays = jnp.where(allowed, jnp.exp(-jnp.where(allowed, spread, 0.0)), 0.0)
    intersection = jnp.einsum(
        "bktgn,bksgn->bkgts", readers, writers, preferred_element_type=f32
    )
    intersection = jnp.repeat(intersection, repeat, axis=2)
    dt_h = jnp.moveaxis(dt, 3, 2)
    mixing = (decays * intersection * dt_h[:, :, :, None, :]).astype(bf16)
    within = jnp.einsum(
        "bkhts,bkshp->bkthp", mixing, x, preferred_element_type=f32
    )

    last_doc = docs[:, :, -1]
    ending = cum[:, :, -1:, :] - cum
    tailing = jnp.where((docs == last_doc[:, :, None])[..., None], jnp.exp(-ending), 0.0) * dt
    scaled = (tailing[..., None] * x.astype(f32)).astype(bf16)
    scaled = scaled.reshape(batches, count, SPAN, groups, repeat, P_SIZE)
    written = jnp.einsum(
        "bksgrp,bksgn->bkgrpn", scaled, writers, preferred_element_type=f32
    )
    totals = cum[:, :, -1, :]

    state = written[:, 0]
    block_outs = [within[:, 0]]
    for index in range(1, count):
        living = (docs[:, index] == last_doc[:, index - 1][:, None]).astype(f32)
        carried = jnp.einsum(
            "btgn,bgrpn->btgrp",
            readers[:, index],
            state.astype(bf16),
            preferred_element_type=f32,
        ).reshape(batches, SPAN, heads, P_SIZE)
        carried = carried * (jnp.exp(-cum[:, index]) * living[:, :, None])[..., None]
        block_outs.append(within[:, index] + carried)
        keeping = jnp.exp(-totals[:, index]) * (
            last_doc[:, index] == last_doc[:, index - 1]
        ).astype(f32)[:, None]
        state = state * keeping.reshape(batches, groups, repeat)[..., None, None] + written[:, index]
    local_out = jnp.stack(block_outs, axis=1).reshape(batches, length, heads, P_SIZE)

    cumulative = jnp.cumsum(step_sizes * decay_rates, axis=1)
    first_doc = doc_ids[:, 0]
    end_doc = doc_ids[:, -1]
    passing = jnp.exp(-cumulative[:, -1, :]) * (first_doc == end_doc).astype(f32)[:, None]
    own_state = state.reshape(batches, heads, P_SIZE, N)
    small = jnp.concatenate(
        [passing, first_doc.astype(f32)[:, None], end_doc.astype(f32)[:, None]], axis=1
    )
    def send(summary, by):
        tiny = jnp.concatenate([summary[0], summary[2][:, None], summary[3][:, None]], axis=1)
        got_small, got_state = shifted((tiny, summary[1].astype(bf16)), "ctx", by)
        return (got_small[:, :heads], got_state.astype(f32), got_small[:, heads], got_small[:, heads + 1])

    own = (passing, own_state, first_doc.astype(f32), end_doc.astype(f32))
    one_back = send(own, 1)
    two_back = send(own, 2)
    three_to_here = link_states(link_states(two_back, one_back), own)
    before = link_states(send(three_to_here, 2), one_back)

    living = (doc_ids.astype(f32) == before[3][:, None]).astype(f32)
    carried = jnp.einsum(
        "btgn,bgrpn->btgrp",
        state_out.reshape(batches, length, groups, N),
        before[1].astype(bf16).reshape(batches, groups, repeat, P_SIZE, N),
        preferred_element_type=f32,
    ).reshape(batches, length, heads, P_SIZE)
    carried = carried * (jnp.exp(-cumulative) * living[:, :, None])[..., None]
    inputs = mixer_input.reshape(batches, length, heads, P_SIZE)
    mixed = local_out + carried + skip_gain[:, None] * inputs.astype(f32)
    gated = mixed.reshape(batches, length, channels) * jax.nn.silu(gate_input.astype(f32))
    shaped = gated.reshape(batches, length, groups, channels // groups)
    factor = lax.rsqrt(jnp.mean(shaped * shaped, axis=-1, keepdims=True) + epsilon)
    normed = ((shaped * factor).reshape(batches, length, channels) * norm_gain).astype(bf16)
    projected = jnp.einsum(
        "btc,cd->btd",
        normed,
        lax.all_gather(out_weight, "ctx", axis=1, tiled=True),
        preferred_element_type=f32,
    )
    mixer_out = lax.psum_scatter(
        projected.astype(bf16), "head", scatter_dimension=2, tiled=True
    )

    kv_heads = keys.shape[2] // HD
    q_repeat = queries.shape[2] // HD // kv_heads
    query_heads = queries.reshape(batches, length, kv_heads, q_repeat, HD)
    window_keys = jnp.concatenate([a[0] for a in arrivals] + [keys], axis=1)
    window_values = jnp.concatenate([a[1] for a in arrivals] + [values], axis=1)
    key_docs = []
    for index, item in enumerate(arrivals):
        offset = reach - index
        key_docs.append(jnp.where(position >= offset, item[2].astype(jnp.int32), -1))
    key_docs = jnp.concatenate(key_docs + [doc_ids], axis=1)
    window = (reach + 1) * length
    query_pos = reach * length + jnp.arange(length, dtype=jnp.int32)
    key_pos = jnp.arange(window, dtype=jnp.int32)
    key_heads = window_keys.reshape(batches, window, kv_heads, HD)
    value_heads = window_values.reshape(batches, window, kv_heads, HD)
    scale = HD ** (-0.5)
    scores = (
        jnp.einsum("bqgrd,bkgd->bgrqk", query_heads, key_heads, preferred_element_type=f32)
        * scale
    )
    allowed = (key_pos[None, :] <= query_pos[:, None])[None] & (
        key_docs[:, None, :] == doc_ids[:, :, None]
    )
    allowed = allowed[:, None, None]
    top = jnp.max(jnp.where(allowed, scores, lowest), axis=-1, keepdims=True)
    probs = jnp.where(allowed, jnp.exp(scores - top), 0.0)
    total = jnp.sum(probs, axis=-1)
    mixed_values = jnp.einsum(
        "bgrqk,bkgd->bgrqd", probs.astype(bf16), value_heads, preferred_element_type=f32
    )
    result = mixed_values / total[..., None]
    attn_out = (
        jnp.transpose(result, (0, 3, 1, 2, 4))
        .reshape(batches, length, kv_heads * q_repeat * HD)
        .astype(bf16)
    )
    return (mixer_out, attn_out)


def solution(mesh):
    in_specs = (
        P(None, "ctx", "head"),
        P(None, "ctx", "head"),
        P(None, "ctx", "head"),
        P(None, "ctx", "head"),
        P(None, "ctx", "head"),
        P("head"),
        P("head"),
        P("head"),
        P("head", "ctx"),
        P(None, "ctx", "head"),
        P(None, "ctx", "head"),
        P(None, "ctx", "head"),
        P(None, "ctx"),
    )
    out_specs = (P(None, "ctx", "head"), P(None, "ctx", "head"))
    return jax.shard_map(shards, mesh=mesh, in_specs=in_specs, out_specs=out_specs, check_vma=False)
```

```python
import jax
import jax.numpy as jnp
from jax import lax
from jax.sharding import PartitionSpec as P

P_SIZE = 64
N = 128
HD = 128
SPAN = 128


epsilon = 1e-05
lowest = -1e30


def shifted(value, axis, by):
    devices = lax.axis_size(axis)
    pairs = [(i, i + by) for i in range(devices) if 0 <= i + by < devices]
    return lax.ppermute(value, axis, pairs)


def link_states(earlier, later):
    decay_one, state_one, first_one, last_one = earlier
    decay_two, state_two, first_two, last_two = later
    passes = ((last_one == first_two) | (last_one < 0.0) | (first_two < 0.0)).astype(jnp.float32)
    through = passes[:, None] * decay_two
    decay = decay_one * through
    state = state_two + through[:, :, None, None] * state_one
    first = jnp.where(first_one < 0.0, first_two, first_one)
    last = jnp.where(last_two < 0.0, last_one, last_two)
    return (decay, state, first, last)


def attention(queries, keys, values, arrivals, doc_ids, position, reach):
    f32 = jnp.float32
    bf16 = jnp.bfloat16
    batches, length = doc_ids.shape
    kv_heads = keys.shape[2] // HD
    q_repeat = queries.shape[2] // HD // kv_heads
    query_heads = queries.reshape(batches, length, kv_heads, q_repeat, HD)
    window_keys = jnp.concatenate([a[0] for a in arrivals] + [keys], axis=1)
    window_values = jnp.concatenate([a[1] for a in arrivals] + [values], axis=1)
    key_docs = []
    for index, item in enumerate(arrivals):
        offset = reach - index
        key_docs.append(jnp.where(position >= offset, item[2].astype(jnp.int32), -1))
    key_docs = jnp.concatenate(key_docs + [doc_ids], axis=1)
    window = (reach + 1) * length
    query_pos = reach * length + jnp.arange(length, dtype=jnp.int32)
    key_pos = jnp.arange(window, dtype=jnp.int32)
    key_heads = window_keys.reshape(batches, window, kv_heads, HD)
    value_heads = window_values.reshape(batches, window, kv_heads, HD)
    scale = HD ** (-0.5)
    scores = (
        jnp.einsum("bqgrd,bkgd->bgrqk", query_heads, key_heads, preferred_element_type=f32)
        * scale
    )
    allowed = (key_pos[None, :] <= query_pos[:, None])[None] & (
        key_docs[:, None, :] == doc_ids[:, :, None]
    )
    allowed = allowed[:, None, None]
    top = jnp.max(jnp.where(allowed, scores, lowest), axis=-1, keepdims=True)
    probs = jnp.where(allowed, jnp.exp(scores - top), 0.0)
    total = jnp.sum(probs, axis=-1)
    mixed_values = jnp.einsum(
        "bgrqk,bkgd->bgrqd", probs.astype(bf16), value_heads, preferred_element_type=f32
    )
    result = mixed_values / total[..., None]
    attn_out = (
        jnp.transpose(result, (0, 3, 1, 2, 4))
        .reshape(batches, length, kv_heads * q_repeat * HD)
        .astype(bf16)
    )
    return attn_out


def shards(
    mixer_input,
    gate_input,
    state_in,
    state_out,
    step_sizes,
    decay_rates,
    skip_gain,
    norm_gain,
    out_weight,
    queries,
    keys,
    values,
    doc_ids,
):
    f32 = jnp.float32
    bf16 = jnp.bfloat16
    batches, length, channels = mixer_input.shape
    heads = step_sizes.shape[2]
    groups = state_in.shape[2] // N
    repeat = heads // groups
    count = length // SPAN
    reach = lax.axis_size("ctx") // 8
    position = lax.axis_index("ctx")

    width = keys.shape[2]
    doc_row = jnp.pad(doc_ids.astype(bf16), ((0, 0), (0, width)))[:, None, :]
    payload = jnp.concatenate([jnp.concatenate([keys, values], axis=2), doc_row], axis=1)
    arrivals = []
    for offset in range(reach, 0, -1):
        got = shifted(payload, "ctx", offset)
        arrivals.append((got[:, :length, :width], got[:, :length, width:], got[:, length, :length]))

    attn_out = attention(queries, keys, values, arrivals, doc_ids, position, reach)
    attn_out, out_weight, mixer_input, gate_input, state_in, state_out, step_sizes = (
        lax.optimization_barrier(
            (attn_out, out_weight, mixer_input, gate_input, state_in, state_out, step_sizes)
        )
    )

    x = mixer_input.reshape(batches, count, SPAN, heads, P_SIZE)
    dt = step_sizes.reshape(batches, count, SPAN, heads)
    docs = doc_ids.reshape(batches, count, SPAN)
    writers = state_in.reshape(batches, count, SPAN, groups, N)
    readers = state_out.reshape(batches, count, SPAN, groups, N)
    cum = jnp.cumsum(dt * decay_rates, axis=2)
    order = jnp.arange(SPAN, dtype=jnp.int32)
    causal = order[:, None] >= order[None, :]
    allowed = ((docs[:, :, :, None] == docs[:, :, None, :]) & causal)[:, :, None]
    cum_h = jnp.moveaxis(cum, 3, 2)
    spread = cum_h[..., :, None] - cum_h[..., None, :]
    decays = jnp.where(allowed, jnp.exp(-jnp.where(allowed, spread, 0.0)), 0.0)
    intersection = jnp.einsum(
        "bktgn,bksgn->bkgts", readers, writers, preferred_element_type=f32
    )
    intersection = jnp.repeat(intersection, repeat, axis=2)
    dt_h = jnp.moveaxis(dt, 3, 2)
    mixing = (decays * intersection * dt_h[:, :, :, None, :]).astype(bf16)
    within = jnp.einsum(
        "bkhts,bkshp->bkthp", mixing, x, preferred_element_type=f32
    )

    last_doc = docs[:, :, -1]
    ending = cum[:, :, -1:, :] - cum
    tailing = jnp.where((docs == last_doc[:, :, None])[..., None], jnp.exp(-ending), 0.0) * dt
    scaled = (tailing[..., None] * x.astype(f32)).astype(bf16)
    scaled = scaled.reshape(batches, count, SPAN, groups, repeat, P_SIZE)
    written = jnp.einsum(
        "bksgrp,bksgn->bkgrpn", scaled, writers, preferred_element_type=f32
    )
    totals = cum[:, :, -1, :]

    state = written[:, 0]
    block_outs = [within[:, 0]]
    for index in range(1, count):
        living = (docs[:, index] == last_doc[:, index - 1][:, None]).astype(f32)
        carried = jnp.einsum(
            "btgn,bgrpn->btgrp",
            readers[:, index],
            state.astype(bf16),
            preferred_element_type=f32,
        ).reshape(batches, SPAN, heads, P_SIZE)
        carried = carried * (jnp.exp(-cum[:, index]) * living[:, :, None])[..., None]
        block_outs.append(within[:, index] + carried)
        keeping = jnp.exp(-totals[:, index]) * (
            last_doc[:, index] == last_doc[:, index - 1]
        ).astype(f32)[:, None]
        state = state * keeping.reshape(batches, groups, repeat)[..., None, None] + written[:, index]
    local_out = jnp.stack(block_outs, axis=1).reshape(batches, length, heads, P_SIZE)

    cumulative = jnp.cumsum(step_sizes * decay_rates, axis=1)
    first_doc = doc_ids[:, 0]
    end_doc = doc_ids[:, -1]
    passing = jnp.exp(-cumulative[:, -1, :]) * (first_doc == end_doc).astype(f32)[:, None]
    own_state = state.reshape(batches, heads, P_SIZE, N)
    small = jnp.concatenate(
        [passing, first_doc.astype(f32)[:, None], end_doc.astype(f32)[:, None]], axis=1
    )
    def send(summary, by):
        tiny = jnp.concatenate([summary[0], summary[2][:, None], summary[3][:, None]], axis=1)
        got_small, got_state = shifted((tiny, summary[1].astype(bf16)), "ctx", by)
        return (got_small[:, :heads], got_state.astype(f32), got_small[:, heads], got_small[:, heads + 1])

    own = (passing, own_state, first_doc.astype(f32), end_doc.astype(f32))
    one_back = send(own, 1)
    two_back = send(own, 2)
    three_to_here = link_states(link_states(two_back, one_back), own)
    before = link_states(send(three_to_here, 2), one_back)

    living = (doc_ids.astype(f32) == before[3][:, None]).astype(f32)
    carried = jnp.einsum(
        "btgn,bgrpn->btgrp",
        state_out.reshape(batches, length, groups, N),
        before[1].astype(bf16).reshape(batches, groups, repeat, P_SIZE, N),
        preferred_element_type=f32,
    ).reshape(batches, length, heads, P_SIZE)
    carried = carried * (jnp.exp(-cumulative) * living[:, :, None])[..., None]
    inputs = mixer_input.reshape(batches, length, heads, P_SIZE)
    mixed = local_out + carried + skip_gain[:, None] * inputs.astype(f32)
    gated = mixed.reshape(batches, length, channels) * jax.nn.silu(gate_input.astype(f32))
    shaped = gated.reshape(batches, length, groups, channels // groups)
    factor = lax.rsqrt(jnp.mean(shaped * shaped, axis=-1, keepdims=True) + epsilon)
    normed = ((shaped * factor).reshape(batches, length, channels) * norm_gain).astype(bf16)
    projected = jnp.einsum(
        "btc,cd->btd",
        normed,
        lax.all_gather(out_weight, "ctx", axis=1, tiled=True),
        preferred_element_type=f32,
    )
    mixer_out = lax.psum_scatter(
        projected.astype(bf16), "head", scatter_dimension=2, tiled=True
    )

    return (mixer_out, attn_out)


def solution(mesh):
    in_specs = (
        P(None, "ctx", "head"),
        P(None, "ctx", "head"),
        P(None, "ctx", "head"),
        P(None, "ctx", "head"),
        P(None, "ctx", "head"),
        P("head"),
        P("head"),
        P("head"),
        P("head", "ctx"),
        P(None, "ctx", "head"),
        P(None, "ctx", "head"),
        P(None, "ctx", "head"),
        P(None, "ctx"),
    )
    out_specs = (P(None, "ctx", "head"), P(None, "ctx", "head"))
    return jax.shard_map(shards, mesh=mesh, in_specs=in_specs, out_specs=out_specs, check_vma=False)
```

```python
import jax
import jax.numpy as jnp
from jax import lax
from jax.sharding import PartitionSpec as P

P_SIZE = 64
N = 128
HD = 128
SPAN = 128


epsilon = 1e-05
lowest = -1e30


def shifted(value, axis, by):
    devices = lax.axis_size(axis)
    pairs = [(i, i + by) for i in range(devices) if 0 <= i + by < devices]
    return lax.ppermute(value, axis, pairs)


def link_states(earlier, later):
    decay_one, state_one, first_one, last_one = earlier
    decay_two, state_two, first_two, last_two = later
    passes = ((last_one == first_two) | (last_one < 0.0) | (first_two < 0.0)).astype(jnp.float32)
    through = passes[:, None] * decay_two
    decay = decay_one * through
    state = state_two + through[:, :, None, None] * state_one
    first = jnp.where(first_one < 0.0, first_two, first_one)
    last = jnp.where(last_two < 0.0, last_one, last_two)
    return (decay, state, first, last)


def shards(
    mixer_input,
    gate_input,
    state_in,
    state_out,
    step_sizes,
    decay_rates,
    skip_gain,
    norm_gain,
    out_weight,
    queries,
    keys,
    values,
    doc_ids,
):
    f32 = jnp.float32
    bf16 = jnp.bfloat16
    batches, length, channels = mixer_input.shape
    heads = step_sizes.shape[2]
    groups = state_in.shape[2] // N
    repeat = heads // groups
    count = length // SPAN
    reach = lax.axis_size("ctx") // 8
    position = lax.axis_index("ctx")

    width = keys.shape[2]
    doc_row = jnp.pad(doc_ids.astype(bf16), ((0, 0), (0, width)))[:, None, :]
    payload = jnp.concatenate([jnp.concatenate([keys, values], axis=2), doc_row], axis=1)

    x = mixer_input.reshape(batches, count, SPAN, heads, P_SIZE)
    dt = step_sizes.reshape(batches, count, SPAN, heads)
    docs = doc_ids.reshape(batches, count, SPAN)
    writers = state_in.reshape(batches, count, SPAN, groups, N)
    readers = state_out.reshape(batches, count, SPAN, groups, N)
    cum = jnp.cumsum(dt * decay_rates, axis=2)
    order = jnp.arange(SPAN, dtype=jnp.int32)
    causal = order[:, None] >= order[None, :]
    allowed = ((docs[:, :, :, None] == docs[:, :, None, :]) & causal)[:, :, None]
    cum_h = jnp.moveaxis(cum, 3, 2)
    spread = cum_h[..., :, None] - cum_h[..., None, :]
    decays = jnp.where(allowed, jnp.exp(-jnp.where(allowed, spread, 0.0)), 0.0)
    intersection = jnp.einsum(
        "bktgn,bksgn->bkgts", readers, writers, preferred_element_type=f32
    )
    intersection = jnp.repeat(intersection, repeat, axis=2)
    dt_h = jnp.moveaxis(dt, 3, 2)
    mixing = (decays * intersection * dt_h[:, :, :, None, :]).astype(bf16)
    within = jnp.einsum(
        "bkhts,bkshp->bkthp", mixing, x, preferred_element_type=f32
    )

    last_doc = docs[:, :, -1]
    ending = cum[:, :, -1:, :] - cum
    tailing = jnp.where((docs == last_doc[:, :, None])[..., None], jnp.exp(-ending), 0.0) * dt
    scaled = (tailing[..., None] * x.astype(f32)).astype(bf16)
    scaled = scaled.reshape(batches, count, SPAN, groups, repeat, P_SIZE)
    written = jnp.einsum(
        "bksgrp,bksgn->bkgrpn", scaled, writers, preferred_element_type=f32
    )
    totals = cum[:, :, -1, :]

    state = written[:, 0]
    block_outs = [within[:, 0]]
    for index in range(1, count):
        living = (docs[:, index] == last_doc[:, index - 1][:, None]).astype(f32)
        carried = jnp.einsum(
            "btgn,bgrpn->btgrp",
            readers[:, index],
            state.astype(bf16),
            preferred_element_type=f32,
        ).reshape(batches, SPAN, heads, P_SIZE)
        carried = carried * (jnp.exp(-cum[:, index]) * living[:, :, None])[..., None]
        block_outs.append(within[:, index] + carried)
        keeping = jnp.exp(-totals[:, index]) * (
            last_doc[:, index] == last_doc[:, index - 1]
        ).astype(f32)[:, None]
        state = state * keeping.reshape(batches, groups, repeat)[..., None, None] + written[:, index]
    local_out = jnp.stack(block_outs, axis=1).reshape(batches, length, heads, P_SIZE)

    cumulative = jnp.cumsum(step_sizes * decay_rates, axis=1)
    first_doc = doc_ids[:, 0]
    end_doc = doc_ids[:, -1]
    passing = jnp.exp(-cumulative[:, -1, :]) * (first_doc == end_doc).astype(f32)[:, None]
    own_state = state.reshape(batches, heads, P_SIZE, N)
    small = jnp.concatenate(
        [passing, first_doc.astype(f32)[:, None], end_doc.astype(f32)[:, None]], axis=1
    )
    def send(summary, by):
        tiny = jnp.concatenate([summary[0], summary[2][:, None], summary[3][:, None]], axis=1)
        got_small, got_state = shifted((tiny, summary[1].astype(bf16)), "ctx", by)
        return (got_small[:, :heads], got_state.astype(f32), got_small[:, heads], got_small[:, heads + 1])

    own = (passing, own_state, first_doc.astype(f32), end_doc.astype(f32))
    one_back = send(own, 1)
    two_back = send(own, 2)
    three_to_here = link_states(link_states(two_back, one_back), own)
    payload, three_state = lax.optimization_barrier((payload, three_to_here[1]))
    three_to_here = (three_to_here[0], three_state, three_to_here[2], three_to_here[3])
    arrivals = []
    for offset in range(reach, 0, -1):
        got = shifted(payload, "ctx", offset)
        arrivals.append((got[:, :length, :width], got[:, :length, width:], got[:, length, :length]))
    before = link_states(send(three_to_here, 2), one_back)

    living = (doc_ids.astype(f32) == before[3][:, None]).astype(f32)
    carried = jnp.einsum(
        "btgn,bgrpn->btgrp",
        state_out.reshape(batches, length, groups, N),
        before[1].astype(bf16).reshape(batches, groups, repeat, P_SIZE, N),
        preferred_element_type=f32,
    ).reshape(batches, length, heads, P_SIZE)
    carried = carried * (jnp.exp(-cumulative) * living[:, :, None])[..., None]
    inputs = mixer_input.reshape(batches, length, heads, P_SIZE)
    mixed = local_out + carried + skip_gain[:, None] * inputs.astype(f32)
    gated = mixed.reshape(batches, length, channels) * jax.nn.silu(gate_input.astype(f32))
    shaped = gated.reshape(batches, length, groups, channels // groups)
    factor = lax.rsqrt(jnp.mean(shaped * shaped, axis=-1, keepdims=True) + epsilon)
    normed = ((shaped * factor).reshape(batches, length, channels) * norm_gain).astype(bf16)
    normed, arrivals = lax.optimization_barrier((normed, arrivals))
    projected = jnp.einsum(
        "btc,cd->btd",
        normed,
        lax.all_gather(out_weight, "ctx", axis=1, tiled=True),
        preferred_element_type=f32,
    )
    mixer_out = lax.psum_scatter(
        projected.astype(bf16), "head", scatter_dimension=2, tiled=True
    )

    kv_heads = keys.shape[2] // HD
    q_repeat = queries.shape[2] // HD // kv_heads
    query_heads = queries.reshape(batches, length, kv_heads, q_repeat, HD)
    window_keys = jnp.concatenate([a[0] for a in arrivals] + [keys], axis=1)
    window_values = jnp.concatenate([a[1] for a in arrivals] + [values], axis=1)
    key_docs = []
    for index, item in enumerate(arrivals):
        offset = reach - index
        key_docs.append(jnp.where(position >= offset, item[2].astype(jnp.int32), -1))
    key_docs = jnp.concatenate(key_docs + [doc_ids], axis=1)
    window = (reach + 1) * length
    query_pos = reach * length + jnp.arange(length, dtype=jnp.int32)
    key_pos = jnp.arange(window, dtype=jnp.int32)
    key_heads = window_keys.reshape(batches, window, kv_heads, HD)
    value_heads = window_values.reshape(batches, window, kv_heads, HD)
    scale = HD ** (-0.5)
    scores = (
        jnp.einsum("bqgrd,bkgd->bgrqk", query_heads, key_heads, preferred_element_type=f32)
        * scale
    )
    allowed = (key_pos[None, :] <= query_pos[:, None])[None] & (
        key_docs[:, None, :] == doc_ids[:, :, None]
    )
    allowed = allowed[:, None, None]
    top = jnp.max(jnp.where(allowed, scores, lowest), axis=-1, keepdims=True)
    probs = jnp.where(allowed, jnp.exp(scores - top), 0.0)
    total = jnp.sum(probs, axis=-1)
    mixed_values = jnp.einsum(
        "bgrqk,bkgd->bgrqd", probs.astype(bf16), value_heads, preferred_element_type=f32
    )
    result = mixed_values / total[..., None]
    attn_out = (
        jnp.transpose(result, (0, 3, 1, 2, 4))
        .reshape(batches, length, kv_heads * q_repeat * HD)
        .astype(bf16)
    )
    return (mixer_out, attn_out)


def solution(mesh):
    in_specs = (
        P(None, "ctx", "head"),
        P(None, "ctx", "head"),
        P(None, "ctx", "head"),
        P(None, "ctx", "head"),
        P(None, "ctx", "head"),
        P("head"),
        P("head"),
        P("head"),
        P("head", "ctx"),
        P(None, "ctx", "head"),
        P(None, "ctx", "head"),
        P(None, "ctx", "head"),
        P(None, "ctx"),
    )
    out_specs = (P(None, "ctx", "head"), P(None, "ctx", "head"))
    return jax.shard_map(shards, mesh=mesh, in_specs=in_specs, out_specs=out_specs, check_vma=False)
```

```python
import jax
import jax.numpy as jnp
from jax import lax
from jax.sharding import PartitionSpec as P

P_SIZE = 64
N = 128
HD = 128
SPAN = 128


epsilon = 1e-05
lowest = -1e30


def shifted(value, axis, by):
    devices = lax.axis_size(axis)
    pairs = [(i, i + by) for i in range(devices) if 0 <= i + by < devices]
    return lax.ppermute(value, axis, pairs)


def link_states(earlier, later):
    decay_one, state_one, first_one, last_one = earlier
    decay_two, state_two, first_two, last_two = later
    passes = ((last_one == first_two) | (last_one < 0.0) | (first_two < 0.0)).astype(jnp.float32)
    through = passes[:, None] * decay_two
    decay = decay_one * through
    state = state_two + through[:, :, None, None] * state_one
    first = jnp.where(first_one < 0.0, first_two, first_one)
    last = jnp.where(last_two < 0.0, last_one, last_two)
    return (decay, state, first, last)


def shards(
    mixer_input,
    gate_input,
    state_in,
    state_out,
    step_sizes,
    decay_rates,
    skip_gain,
    norm_gain,
    out_weight,
    queries,
    keys,
    values,
    doc_ids,
):
    f32 = jnp.float32
    bf16 = jnp.bfloat16
    batches, length, channels = mixer_input.shape
    heads = step_sizes.shape[2]
    groups = state_in.shape[2] // N
    repeat = heads // groups
    count = length // SPAN
    reach = lax.axis_size("ctx") // 8
    position = lax.axis_index("ctx")

    width = keys.shape[2]
    doc_row = jnp.pad(doc_ids.astype(bf16), ((0, 0), (0, width)))[:, None, :]
    payload = jnp.concatenate([jnp.concatenate([keys, values], axis=2), doc_row], axis=1)

    x = mixer_input.reshape(batches, count, SPAN, heads, P_SIZE)
    dt = step_sizes.reshape(batches, count, SPAN, heads)
    docs = doc_ids.reshape(batches, count, SPAN)
    writers = state_in.reshape(batches, count, SPAN, groups, N)
    readers = state_out.reshape(batches, count, SPAN, groups, N)
    cum = jnp.cumsum(dt * decay_rates, axis=2)
    order = jnp.arange(SPAN, dtype=jnp.int32)
    causal = order[:, None] >= order[None, :]
    allowed = ((docs[:, :, :, None] == docs[:, :, None, :]) & causal)[:, :, None]
    cum_h = jnp.moveaxis(cum, 3, 2)
    spread = cum_h[..., :, None] - cum_h[..., None, :]
    decays = jnp.where(allowed, jnp.exp(-jnp.where(allowed, spread, 0.0)), 0.0)
    intersection = jnp.einsum(
        "bktgn,bksgn->bkgts", readers, writers, preferred_element_type=f32
    )
    intersection = jnp.repeat(intersection, repeat, axis=2)
    dt_h = jnp.moveaxis(dt, 3, 2)
    mixing = (decays * intersection * dt_h[:, :, :, None, :]).astype(bf16)
    within = jnp.einsum(
        "bkhts,bkshp->bkthp", mixing, x, preferred_element_type=f32
    )

    last_doc = docs[:, :, -1]
    ending = cum[:, :, -1:, :] - cum
    tailing = jnp.where((docs == last_doc[:, :, None])[..., None], jnp.exp(-ending), 0.0) * dt
    scaled = (tailing[..., None] * x.astype(f32)).astype(bf16)
    scaled = scaled.reshape(batches, count, SPAN, groups, repeat, P_SIZE)
    written = jnp.einsum(
        "bksgrp,bksgn->bkgrpn", scaled, writers, preferred_element_type=f32
    )
    totals = cum[:, :, -1, :]

    state = written[:, 0]
    block_outs = [within[:, 0]]
    for index in range(1, count):
        living = (docs[:, index] == last_doc[:, index - 1][:, None]).astype(f32)
        carried = jnp.einsum(
            "btgn,bgrpn->btgrp",
            readers[:, index],
            state.astype(bf16),
            preferred_element_type=f32,
        ).reshape(batches, SPAN, heads, P_SIZE)
        carried = carried * (jnp.exp(-cum[:, index]) * living[:, :, None])[..., None]
        block_outs.append(within[:, index] + carried)
        keeping = jnp.exp(-totals[:, index]) * (
            last_doc[:, index] == last_doc[:, index - 1]
        ).astype(f32)[:, None]
        state = state * keeping.reshape(batches, groups, repeat)[..., None, None] + written[:, index]
    local_out = jnp.stack(block_outs, axis=1).reshape(batches, length, heads, P_SIZE)

    cumulative = jnp.cumsum(step_sizes * decay_rates, axis=1)
    first_doc = doc_ids[:, 0]
    end_doc = doc_ids[:, -1]
    passing = jnp.exp(-cumulative[:, -1, :]) * (first_doc == end_doc).astype(f32)[:, None]
    own_state = state.reshape(batches, heads, P_SIZE, N)
    small = jnp.concatenate(
        [passing, first_doc.astype(f32)[:, None], end_doc.astype(f32)[:, None]], axis=1
    )
    def send(summary, by):
        tiny = jnp.concatenate([summary[0], summary[2][:, None], summary[3][:, None]], axis=1)
        got_small, got_state = shifted((tiny, summary[1].astype(bf16)), "ctx", by)
        return (got_small[:, :heads], got_state.astype(f32), got_small[:, heads], got_small[:, heads + 1])

    own = (passing, own_state, first_doc.astype(f32), end_doc.astype(f32))
    one_back = send(own, 1)
    two_back = send(own, 2)
    three_to_here = link_states(link_states(two_back, one_back), own)
    got_one = shifted(payload, "ctx", 1)
    got_two = shifted(payload, "ctx", 2)
    got_one, got_two, three_state = lax.optimization_barrier((got_one, got_two, three_to_here[1]))
    three_to_here = (three_to_here[0], three_state, three_to_here[2], three_to_here[3])
    got_far = shifted(jnp.concatenate([got_two, got_one], axis=1), "ctx", 2)
    rows = payload.shape[1]
    received_kv = [got_far[:, :rows], got_far[:, rows:], got_two, got_one]
    arrivals = [
        (got[:, :length, :width], got[:, :length, width:], got[:, length, :length]) for got in received_kv
    ]
    before = link_states(send(three_to_here, 2), one_back)

    living = (doc_ids.astype(f32) == before[3][:, None]).astype(f32)
    carried = jnp.einsum(
        "btgn,bgrpn->btgrp",
        state_out.reshape(batches, length, groups, N),
        before[1].astype(bf16).reshape(batches, groups, repeat, P_SIZE, N),
        preferred_element_type=f32,
    ).reshape(batches, length, heads, P_SIZE)
    carried = carried * (jnp.exp(-cumulative) * living[:, :, None])[..., None]
    inputs = mixer_input.reshape(batches, length, heads, P_SIZE)
    mixed = local_out + carried + skip_gain[:, None] * inputs.astype(f32)
    gated = mixed.reshape(batches, length, channels) * jax.nn.silu(gate_input.astype(f32))
    shaped = gated.reshape(batches, length, groups, channels // groups)
    factor = lax.rsqrt(jnp.mean(shaped * shaped, axis=-1, keepdims=True) + epsilon)
    normed = ((shaped * factor).reshape(batches, length, channels) * norm_gain).astype(bf16)
    normed, arrivals = lax.optimization_barrier((normed, arrivals))
    projected = jnp.einsum(
        "btc,cd->btd",
        normed,
        lax.all_gather(out_weight, "ctx", axis=1, tiled=True),
        preferred_element_type=f32,
    )
    mixer_out = lax.psum_scatter(
        projected.astype(bf16), "head", scatter_dimension=2, tiled=True
    )

    kv_heads = keys.shape[2] // HD
    q_repeat = queries.shape[2] // HD // kv_heads
    query_heads = queries.reshape(batches, length, kv_heads, q_repeat, HD)
    window_keys = jnp.concatenate([a[0] for a in arrivals] + [keys], axis=1)
    window_values = jnp.concatenate([a[1] for a in arrivals] + [values], axis=1)
    key_docs = []
    for index, item in enumerate(arrivals):
        offset = reach - index
        key_docs.append(jnp.where(position >= offset, item[2].astype(jnp.int32), -1))
    key_docs = jnp.concatenate(key_docs + [doc_ids], axis=1)
    window = (reach + 1) * length
    query_pos = reach * length + jnp.arange(length, dtype=jnp.int32)
    key_pos = jnp.arange(window, dtype=jnp.int32)
    key_heads = window_keys.reshape(batches, window, kv_heads, HD)
    value_heads = window_values.reshape(batches, window, kv_heads, HD)
    scale = HD ** (-0.5)
    scores = (
        jnp.einsum("bqgrd,bkgd->bgrqk", query_heads, key_heads, preferred_element_type=f32)
        * scale
    )
    allowed = (key_pos[None, :] <= query_pos[:, None])[None] & (
        key_docs[:, None, :] == doc_ids[:, :, None]
    )
    allowed = allowed[:, None, None]
    top = jnp.max(jnp.where(allowed, scores, lowest), axis=-1, keepdims=True)
    probs = jnp.where(allowed, jnp.exp(scores - top), 0.0)
    total = jnp.sum(probs, axis=-1)
    mixed_values = jnp.einsum(
        "bgrqk,bkgd->bgrqd", probs.astype(bf16), value_heads, preferred_element_type=f32
    )
    result = mixed_values / total[..., None]
    attn_out = (
        jnp.transpose(result, (0, 3, 1, 2, 4))
        .reshape(batches, length, kv_heads * q_repeat * HD)
        .astype(bf16)
    )
    return (mixer_out, attn_out)


def solution(mesh):
    in_specs = (
        P(None, "ctx", "head"),
        P(None, "ctx", "head"),
        P(None, "ctx", "head"),
        P(None, "ctx", "head"),
        P(None, "ctx", "head"),
        P("head"),
        P("head"),
        P("head"),
        P("head", "ctx"),
        P(None, "ctx", "head"),
        P(None, "ctx", "head"),
        P(None, "ctx", "head"),
        P(None, "ctx"),
    )
    out_specs = (P(None, "ctx", "head"), P(None, "ctx", "head"))
    return jax.shard_map(shards, mesh=mesh, in_specs=in_specs, out_specs=out_specs, check_vma=False)
```

```python
import jax
import jax.numpy as jnp
from jax import lax
from jax.sharding import PartitionSpec as P

P_SIZE = 64
N = 128
HD = 128
SPAN = 128


epsilon = 1e-05
lowest = -1e30


def shifted(value, axis, by):
    devices = lax.axis_size(axis)
    pairs = [(i, i + by) for i in range(devices) if 0 <= i + by < devices]
    return lax.ppermute(value, axis, pairs)


def link_states(earlier, later):
    decay_one, state_one, first_one, last_one = earlier
    decay_two, state_two, first_two, last_two = later
    passes = ((last_one == first_two) | (last_one < 0.0) | (first_two < 0.0)).astype(jnp.float32)
    through = passes[:, None] * decay_two
    decay = decay_one * through
    state = state_two + through[:, :, None, None] * state_one
    first = jnp.where(first_one < 0.0, first_two, first_one)
    last = jnp.where(last_two < 0.0, last_one, last_two)
    return (decay, state, first, last)


def shards(
    mixer_input,
    gate_input,
    state_in,
    state_out,
    step_sizes,
    decay_rates,
    skip_gain,
    norm_gain,
    out_weight,
    queries,
    keys,
    values,
    doc_ids,
):
    f32 = jnp.float32
    bf16 = jnp.bfloat16
    batches, length, channels = mixer_input.shape
    heads = step_sizes.shape[2]
    groups = state_in.shape[2] // N
    repeat = heads // groups
    count = length // SPAN
    reach = lax.axis_size("ctx") // 8
    position = lax.axis_index("ctx")

    width = keys.shape[2]
    doc_row = jnp.pad(doc_ids.astype(bf16), ((0, 0), (0, width)))[:, None, :]
    payload = jnp.concatenate([jnp.concatenate([keys, values], axis=2), doc_row], axis=1)

    x = mixer_input.reshape(batches, count, SPAN, heads, P_SIZE)
    dt = step_sizes.reshape(batches, count, SPAN, heads)
    docs = doc_ids.reshape(batches, count, SPAN)
    writers = state_in.reshape(batches, count, SPAN, groups, N)
    readers = state_out.reshape(batches, count, SPAN, groups, N)
    cum = jnp.cumsum(dt * decay_rates, axis=2)
    order = jnp.arange(SPAN, dtype=jnp.int32)
    causal = order[:, None] >= order[None, :]
    allowed = ((docs[:, :, :, None] == docs[:, :, None, :]) & causal)[:, :, None]
    cum_h = jnp.moveaxis(cum, 3, 2)
    spread = cum_h[..., :, None] - cum_h[..., None, :]
    decays = jnp.where(allowed, jnp.exp(-jnp.where(allowed, spread, 0.0)), 0.0)
    intersection = jnp.einsum(
        "bktgn,bksgn->bkgts", readers, writers, preferred_element_type=f32
    )
    intersection = jnp.repeat(intersection, repeat, axis=2)
    dt_h = jnp.moveaxis(dt, 3, 2)
    mixing = (decays * intersection * dt_h[:, :, :, None, :]).astype(bf16)
    within = jnp.einsum(
        "bkhts,bkshp->bkthp", mixing, x, preferred_element_type=f32
    )

    last_doc = docs[:, :, -1]
    ending = cum[:, :, -1:, :] - cum
    tailing = jnp.where((docs == last_doc[:, :, None])[..., None], jnp.exp(-ending), 0.0) * dt
    scaled = (tailing[..., None] * x.astype(f32)).astype(bf16)
    scaled = scaled.reshape(batches, count, SPAN, groups, repeat, P_SIZE)
    written = jnp.einsum(
        "bksgrp,bksgn->bkgrpn", scaled, writers, preferred_element_type=f32
    )
    totals = cum[:, :, -1, :]

    state = written[:, 0]
    block_outs = [within[:, 0]]
    for index in range(1, count):
        living = (docs[:, index] == last_doc[:, index - 1][:, None]).astype(f32)
        carried = jnp.einsum(
            "btgn,bgrpn->btgrp",
            readers[:, index],
            state.astype(bf16),
            preferred_element_type=f32,
        ).reshape(batches, SPAN, heads, P_SIZE)
        carried = carried * (jnp.exp(-cum[:, index]) * living[:, :, None])[..., None]
        block_outs.append(within[:, index] + carried)
        keeping = jnp.exp(-totals[:, index]) * (
            last_doc[:, index] == last_doc[:, index - 1]
        ).astype(f32)[:, None]
        state = state * keeping.reshape(batches, groups, repeat)[..., None, None] + written[:, index]
    local_out = jnp.stack(block_outs, axis=1).reshape(batches, length, heads, P_SIZE)

    cumulative = jnp.cumsum(step_sizes * decay_rates, axis=1)
    first_doc = doc_ids[:, 0]
    end_doc = doc_ids[:, -1]
    passing = jnp.exp(-cumulative[:, -1, :]) * (first_doc == end_doc).astype(f32)[:, None]
    own_state = state.reshape(batches, heads, P_SIZE, N)
    small = jnp.concatenate(
        [passing, first_doc.astype(f32)[:, None], end_doc.astype(f32)[:, None]], axis=1
    )
    def send(summary, by):
        tiny = jnp.concatenate([summary[0], summary[2][:, None], summary[3][:, None]], axis=1)
        got_small, got_state = shifted((tiny, summary[1].astype(bf16)), "ctx", by)
        return (got_small[:, :heads], got_state.astype(f32), got_small[:, heads], got_small[:, heads + 1])

    own = (passing, own_state, first_doc.astype(f32), end_doc.astype(f32))
    one_back = send(own, 1)
    two_back = send(own, 2)
    three_to_here = link_states(link_states(two_back, one_back), own)
    got_one = shifted(payload, "ctx", 1)
    got_two = shifted(payload, "ctx", 2)
    got_one, got_two, three_state = lax.optimization_barrier((got_one, got_two, three_to_here[1]))
    three_to_here = (three_to_here[0], three_state, three_to_here[2], three_to_here[3])
    got_far = shifted(jnp.concatenate([got_two, got_one], axis=1), "ctx", 2)
    rows = payload.shape[1]
    received_kv = [got_far[:, :rows], got_far[:, rows:], got_two, got_one]
    arrivals = [
        (got[:, :length, :width], got[:, :length, width:], got[:, length, :length]) for got in received_kv
    ]
    before = link_states(send(three_to_here, 2), one_back)

    living = (doc_ids.astype(f32) == before[3][:, None]).astype(f32)
    carried = jnp.einsum(
        "btgn,bgrpn->btgrp",
        state_out.reshape(batches, length, groups, N),
        before[1].astype(bf16).reshape(batches, groups, repeat, P_SIZE, N),
        preferred_element_type=f32,
    ).reshape(batches, length, heads, P_SIZE)
    carried = carried * (jnp.exp(-cumulative) * living[:, :, None])[..., None]
    inputs = mixer_input.reshape(batches, length, heads, P_SIZE)
    mixed = local_out + carried + skip_gain[:, None] * inputs.astype(f32)
    gated = mixed.reshape(batches, length, channels) * jax.nn.silu(gate_input.astype(f32))
    shaped = gated.reshape(batches, length, groups, channels // groups)
    factor = lax.rsqrt(jnp.mean(shaped * shaped, axis=-1, keepdims=True) + epsilon)
    normed = ((shaped * factor).reshape(batches, length, channels) * norm_gain).astype(bf16)
    normed, arrivals = lax.optimization_barrier((normed, arrivals))
    projected = jnp.einsum(
        "btc,cd->btd",
        normed,
        lax.all_gather(out_weight, "ctx", axis=1, tiled=True),
        preferred_element_type=f32,
    )
    mixer_out = lax.psum_scatter(
        projected.astype(bf16), "head", scatter_dimension=2, tiled=True
    )

    kv_heads = keys.shape[2] // HD
    q_repeat = queries.shape[2] // HD // kv_heads
    query_heads = queries.reshape(batches, length, kv_heads, q_repeat, HD)
    chunks = [(a[0], a[1], jnp.where(position >= reach - i, a[2].astype(jnp.int32), -1))
              for i, a in enumerate(arrivals)] + [(keys, values, doc_ids)]
    query_pos = reach * length + jnp.arange(length, dtype=jnp.int32)
    scale = HD ** (-0.5)

    def part(first, last):
        window = (last - first) * length
        key_heads = jnp.concatenate([c[0] for c in chunks[first:last]], axis=1).reshape(
            batches, window, kv_heads, HD
        )
        value_heads = jnp.concatenate([c[1] for c in chunks[first:last]], axis=1).reshape(
            batches, window, kv_heads, HD
        )
        key_docs = jnp.concatenate([c[2] for c in chunks[first:last]], axis=1)
        key_pos = first * length + jnp.arange(window, dtype=jnp.int32)
        scores = (
            jnp.einsum("bqgrd,bkgd->bgrqk", query_heads, key_heads, preferred_element_type=f32)
            * scale
        )
        allowed = (key_pos[None, :] <= query_pos[:, None])[None] & (
            key_docs[:, None, :] == doc_ids[:, :, None]
        )
        allowed = allowed[:, None, None]
        top = jnp.max(jnp.where(allowed, scores, lowest), axis=-1)
        probs = jnp.where(allowed, jnp.exp(scores - top[..., None]), 0.0)
        total = jnp.sum(probs, axis=-1)
        mixed = jnp.einsum(
            "bgrqk,bkgd->bgrqd", probs.astype(bf16), value_heads, preferred_element_type=f32
        )
        return top, total, mixed

    near = part(reach // 2, reach + 1)
    far = part(0, reach // 2)
    top = jnp.maximum(near[0], far[0])
    near_scale = jnp.exp(near[0] - top)
    far_scale = jnp.exp(far[0] - top)
    total = near[1] * near_scale + far[1] * far_scale
    mixed_values = near[2] * near_scale[..., None] + far[2] * far_scale[..., None]
    result = mixed_values / total[..., None]
    attn_out = (
        jnp.transpose(result, (0, 3, 1, 2, 4))
        .reshape(batches, length, kv_heads * q_repeat * HD)
        .astype(bf16)
    )
    return (mixer_out, attn_out)


def solution(mesh):
    in_specs = (
        P(None, "ctx", "head"),
        P(None, "ctx", "head"),
        P(None, "ctx", "head"),
        P(None, "ctx", "head"),
        P(None, "ctx", "head"),
        P("head"),
        P("head"),
        P("head"),
        P("head", "ctx"),
        P(None, "ctx", "head"),
        P(None, "ctx", "head"),
        P(None, "ctx", "head"),
        P(None, "ctx"),
    )
    out_specs = (P(None, "ctx", "head"), P(None, "ctx", "head"))
    return jax.shard_map(shards, mesh=mesh, in_specs=in_specs, out_specs=out_specs, check_vma=False)
```
